256 devices in a mesh: grp: 8 (over y, x_hi), fsdp: 32 (over z, x_lo, core).
Axes of the slice: x: 4 (x_hi: 2, x_lo: 2; x = x_hi * 2 + x_lo), y: 4, z: 8, core: 2. Of those that a mesh axis runs over, the one named last changes fastest.
Arguments:
- layer_input: bfloat16 [8, 1536, 8192], P('grp', 'fsdp'), may hold values from -6 to 6
- norm_gain: float32 [8, 8192], P('grp'), may hold values from 0.5 to 1.5
- layer_weight: bfloat16 [8, 8192, 12288], P('grp', None, 'fsdp'), may hold values from -1.5 to 1.5
- score_vec: bfloat16 [8, 4096], P('grp', 'fsdp'), may hold values from -0.09375 to 0.09375
- lengths: int32 [8, 8], P('grp'), may hold values from 1 to 384, 1536 in all within a row
- bins: int32 [8, 1536], P('grp', 'fsdp'), may hold values from 0 to 15
- group_map: int32 [4], replicated, may hold values from 0 to 3, each once
- cotangent: bfloat16 [8, 1536, 4096], P('grp', None, 'fsdp'), may hold values from -6 to 6
Outputs:
- ratio_weights: float32 [8, 1536], P('grp', 'fsdp')
- grad: bfloat16 [8, 8192, 4096], P('grp', None, 'fsdp')
The draws below stay inside these ranges and needn't reach their ends.
Inputs may be any that keep to these rules, and one draw needn't show every extreme that they name: Each row holds 8 response lengths that fill 1536 tokens; the longest is exactly 384. `group_map`: A permutation of the classifier groups.
All inputs are finite; a program needn't handle non-finite values.
Results may differ from the reference program's by a relative error of at most 0.0071.
Values may be sent and summed in bfloat16 or wider, within the bound.
No kernel may reach another device: no remote copies, remote signals or barrier semaphores. Data moves between devices by JAX's collectives and lax.ppermute only.
A program may use at most 128 MiB of HBM per device.

```python
import math
import jax
import jax.numpy as jnp
import numpy as np
from jax import lax

D = 8192
HD = 128
NBINS = 16
NRESP = 8
HQ = 32
HK = 4
LEN = 1536
MAXLEN = 384
N_GRP = 8


def draw_layer_input(key, part):
    base = jax.random.normal(key, (N_GRP, LEN, D), jnp.float32)
    return jnp.clip(base, -6.0, 6.0).astype(jnp.bfloat16)


def draw_layer_weight(key, part):
    scale_in = D ** (-0.5)
    query_part = jax.random.normal(jax.random.fold_in(key, 1), (N_GRP, D, HQ, HD), jnp.float32) * scale_in
    key_part = jax.random.normal(jax.random.fold_in(key, 2), (N_GRP, D, HK, HD), jnp.float32) * scale_in
    value_part = jax.random.normal(jax.random.fold_in(key, 3), (N_GRP, D, HK, HD), jnp.float32) * scale_in
    key_rep = jnp.repeat(key_part, 8, axis=2)
    value_rep = jnp.repeat(value_part, 8, axis=2)
    joined = jnp.stack([query_part, key_rep, value_rep], axis=3).reshape(N_GRP, D, HQ * 3 * HD)
    return jnp.clip(joined, -1.5, 1.5).astype(jnp.bfloat16)


def with_ends(entries, stream_key, least, high):
    index_at = [jax.random.randint(jax.random.fold_in(stream_key, axis), (), 0, length) for axis, length in enumerate(entries.shape)]
    widest = entries.shape.index(max(entries.shape))
    next_to = index_at[:widest] + [(index_at[widest] + 1) % entries.shape[widest]] + index_at[widest + 1:]
    return entries.at[tuple(index_at)].set(least).at[tuple(next_to)].set(high)


def levels(rng, extent, pieces, low, largest):
    gain = 1.0
    for dim, parts in pieces:
        heights = jax.random.uniform(jax.random.fold_in(jax.random.fold_in(rng, 6), dim), (parts,), jnp.float32, low / len(pieces), largest / len(pieces))
        gain = gain * jnp.repeat(jnp.exp(heights), extent[dim] // parts).reshape((-1,) + (1,) * (len(extent) - 1 - dim))
    return gain


def length_profile(number_of, total, reach, lean):
    portions = [(1 << 20) // math.isqrt(standing ** lean) + 1 for standing in range(2, number_of + 1)]
    rest, given = total - reach - (number_of - 1), [1] * (number_of - 1)
    while rest > 0:
        free = [i for i in range(number_of - 1) if given[i] < reach]
        mass, budget = sum([portions[i] for i in free]), rest
        for i in free:
            addition = min(reach - given[i], max(1, budget * portions[i] // mass), rest)
            given[i] = given[i] + addition
            rest = rest - addition
    return np.array([reach] + given)


def uneven_parts(stream_key, number_of, total, reach, skew):
    if number_of == 2:
        one = jax.random.randint(stream_key, (), max(1, total - reach), min(reach, total - 1) + 1)
        return jnp.stack([one, total - one])
    sizes = jnp.asarray(length_profile(number_of, total, reach, skew), jnp.int32)
    couples = (number_of - 1) // 2
    donor, receiver = sizes[1:1 + 2 * couples:2], sizes[2:2 + 2 * couples:2]
    room = jnp.minimum(donor - 1, reach - receiver)
    shifted = jax.random.randint(jax.random.fold_in(stream_key, 1), (couples,), 0, 1 << 20) % (room + 1)
    sizes = sizes.at[1:1 + 2 * couples:2].set(donor - shifted).at[2:2 + 2 * couples:2].set(receiver + shifted)
    return sizes[jax.random.permutation(jax.random.fold_in(stream_key, 2), number_of)]


def scatter_about(own_key, shape, width, bound, shards=(), kind=jnp.bfloat16):
    result = width * jax.random.normal(own_key, shape, jnp.float32)
    if shards:
        result = result * levels(own_key, shape, shards, -0.22, 0.18)
    return jnp.clip(result, -bound, bound).astype(kind)


def setup_inputs(seed: int = 0) -> dict:
    seeds = jax.random.split(jax.random.key(seed), 9)
    return {
        "layer_input": draw_layer_input(jax.random.fold_in(seeds[8], 71), 0),
        "norm_gain": jnp.clip(1.0 + 0.1 * jax.random.normal(seeds[1], (N_GRP, D), jnp.float32), 0.5, 1.5),
        "layer_weight": draw_layer_weight(jax.random.fold_in(seeds[8], 71), 0),
        "score_vec": scatter_about(seeds[3], (N_GRP, HQ * HD), (HQ * HD) ** -0.5, 0.09375, ((0, 8), (1, 32))),
        "lengths": jax.vmap(lambda own: uneven_parts(own, NRESP, LEN, MAXLEN, 0))(jax.random.split(seeds[4], N_GRP)).reshape((N_GRP, NRESP)).astype(jnp.int32),
        "bins": with_ends(jax.random.randint(seeds[5], (N_GRP, LEN), 0, NBINS), jax.random.fold_in(seeds[5], 1), 0, NBINS - 1).astype(jnp.int32),
        "group_map": jax.random.permutation(seeds[6], N_GRP // 2).astype(jnp.int32),
        "cotangent": scatter_about(seeds[7], (N_GRP, LEN, HQ * HD), 1.0, 6.0, ((0, 8), (2, 32))),
    }


def normalize_rows(rows_in, scale_row):
    values_f = rows_in.astype(jnp.float32)
    mean_sq = lax.optimization_barrier(jnp.mean(values_f * values_f, axis=-1, keepdims=True))
    return (values_f * lax.rsqrt(mean_sq + 1e-05) * scale_row).astype(jnp.bfloat16)

def segment_ids(length_row, total_len):
    response_ends = jnp.cumsum(length_row).astype(jnp.int32)
    positions = jnp.arange(total_len, dtype=jnp.int32)
    return lax.optimization_barrier(jnp.sum((positions[:, None] >= response_ends[None, :]).astype(jnp.int32), axis=1))

def head_logits(query_rows, key_rows, value_rows, score_row, segment, row_start):
    row_count = query_rows.shape[0]
    head_size = query_rows.shape[1]
    scores = jnp.dot(query_rows, key_rows.T, preferred_element_type=jnp.float32) * head_size ** (-0.5)
    query_pos = row_start + jnp.arange(row_count, dtype=jnp.int32)
    key_pos = jnp.arange(key_rows.shape[0], dtype=jnp.int32)
    query_seg = lax.dynamic_slice_in_dim(segment, row_start, row_count, 0)
    allowed = (query_seg[:, None] == segment[None, :]) & (key_pos[None, :] <= query_pos[:, None])
    scores = jnp.where(allowed, scores, -1e+30)
    highest = lax.optimization_barrier(jnp.max(scores, axis=1, keepdims=True))
    expo = jnp.exp(scores - highest)
    weights = (expo / lax.optimization_barrier(jnp.sum(expo, axis=1, keepdims=True))).astype(jnp.bfloat16)
    mixed = jnp.dot(weights, value_rows, preferred_element_type=jnp.float32)
    return jnp.dot(mixed, score_row, precision=lax.Precision.HIGHEST)

def bin_tables(bin_row):
    return (bin_row[:, None] == jnp.arange(NBINS, dtype=jnp.int32)[None, :]).astype(jnp.float32)

def reference(layer_input, norm_gain, layer_weight, score_vec, lengths, bins, group_map, cotangent):
    half_groups = N_GRP // 2
    classifier_rows = []
    for group_id in range(half_groups):
        normed = normalize_rows(layer_input[group_id], norm_gain[group_id])
        projected = jnp.dot(normed, layer_weight[group_id], preferred_element_type=jnp.float32).astype(jnp.bfloat16)
        projected = projected.reshape(LEN, HQ, 3, HD)
        segment = segment_ids(lengths[group_id], LEN)
        score_heads = score_vec[group_id].astype(jnp.float32).reshape(HQ, HD)

        def one_head(head_id):
            return head_logits(projected[:, head_id, 0], projected[:, head_id, 1], projected[:, head_id, 2], score_heads[head_id], segment, 0)
        logits = lax.optimization_barrier(jnp.sum(lax.map(one_head, jnp.arange(HQ, dtype=jnp.int32)), axis=0))
        onehot = bin_tables(bins[group_id])
        counts = lax.optimization_barrier(jnp.sum(onehot, axis=0))
        sums = jnp.dot(jax.nn.sigmoid(logits), onehot, precision=lax.Precision.HIGHEST)
        calib = (counts - sums + 1.0) / (sums + 1.0)
        ratio = jnp.exp(logits) * jnp.dot(onehot, calib, precision=lax.Precision.HIGHEST)
        classifier_rows.append(ratio * LEN / jnp.sum(ratio))
    classifier_stack = jnp.stack(classifier_rows)
    policy_stack = classifier_stack[group_map]
    grads = [jnp.zeros((D, HQ * HD), jnp.bfloat16) for group_id in range(half_groups)]
    for index_id in range(half_groups):
        group_id = half_groups + index_id
        normed = normalize_rows(layer_input[group_id], norm_gain[group_id])
        weighted = (policy_stack[index_id][:, None] * cotangent[group_id].astype(jnp.float32)).astype(jnp.bfloat16)
        product = jnp.dot(normed.T, weighted, preferred_element_type=jnp.float32)
        grads.append((product * LEN ** (-0.5)).astype(jnp.bfloat16))
    return (jnp.concatenate([classifier_stack, policy_stack], axis=0), jnp.stack(grads))
```

```python
import jax
import jax.numpy as jnp
from jax import lax
from jax.sharding import PartitionSpec as P

NBINS = 16


def normalize_rows(rows_in, scale_row):
    values_f = rows_in.astype(jnp.float32)
    mean_sq = jnp.mean(values_f * values_f, axis=-1, keepdims=True)
    return (values_f * lax.rsqrt(mean_sq + 1e-05) * scale_row).astype(jnp.bfloat16)


def segment_ids(length_row, total_len):
    response_ends = jnp.cumsum(length_row)
    positions = jnp.arange(total_len, dtype=jnp.int32)
    return jnp.sum((positions[:, None] >= response_ends[None, :]).astype(jnp.int32), axis=1)


def head_logits(query_rows, key_rows, value_rows, score_row, segment):
    row_count = query_rows.shape[0]
    head_size = query_rows.shape[1]
    scores = jnp.dot(query_rows, key_rows.T, preferred_element_type=jnp.float32) * head_size ** (
        -0.5
    )
    query_pos = jnp.arange(row_count, dtype=jnp.int32)
    key_pos = jnp.arange(key_rows.shape[0], dtype=jnp.int32)
    allowed = (segment[:, None] == segment[None, :]) & (key_pos[None, :] <= query_pos[:, None])
    scores = jnp.where(allowed, scores, -1e30)
    highest = jnp.max(scores, axis=1, keepdims=True)
    expo = jnp.exp(scores - highest)
    weights = (expo / jnp.sum(expo, axis=1, keepdims=True)).astype(jnp.bfloat16)
    mixed = jnp.dot(weights, value_rows, preferred_element_type=jnp.float32)
    return jnp.dot(mixed, score_row, precision=lax.Precision.HIGHEST)


def group_weights(logits, bin_row, total_len):
    onehot = (bin_row[:, None] == jnp.arange(NBINS, dtype=jnp.int32)[None, :]).astype(jnp.float32)
    counts = jnp.sum(onehot, axis=0)
    sums = jnp.dot(jax.nn.sigmoid(logits), onehot, precision=lax.Precision.HIGHEST)
    calib = (counts - sums + 1.0) / (sums + 1.0)
    ratio = jnp.exp(logits) * jnp.dot(onehot, calib, precision=lax.Precision.HIGHEST)
    return ratio * total_len / jnp.sum(ratio)


def per_device(
    layer_input, norm_gain, layer_weight, score_vec, lengths, bins, group_map, cotangent
):
    n_groups = lax.axis_size("grp")
    half_groups = n_groups // 2
    my_group = lax.axis_index("grp")
    classify = my_group < half_groups
    bins_all = lax.all_gather(bins[0], ("grp", "fsdp"), axis=0, tiled=True).reshape(
        n_groups, -1
    )
    normed = lax.all_gather(
        normalize_rows(layer_input[0], norm_gain[0]), "fsdp", axis=0, tiled=True
    )
    total_len = normed.shape[0]
    head_size = layer_weight.shape[2] // 3
    segment = segment_ids(lengths[0], total_len)
    score_row = score_vec[0].astype(jnp.float32)
    local_rows = bins.shape[1]

    def attend():
        projected = jnp.dot(
            normed, layer_weight[0], preferred_element_type=jnp.float32
        ).astype(jnp.bfloat16)
        return head_logits(
            projected[:, :head_size],
            projected[:, head_size : 2 * head_size],
            projected[:, 2 * head_size :],
            score_row,
            segment,
        )

    def skipped():
        return jnp.zeros((total_len,), jnp.float32)

    contrib = lax.cond(classify, attend, skipped)
    slot = jnp.arange(half_groups, dtype=jnp.int32)[:, None] == my_group
    logits_all = lax.psum(jnp.where(slot, contrib[None, :], 0.0), ("grp", "fsdp"))
    policy_index = jnp.clip(my_group - half_groups, 0, half_groups - 1)
    source = jnp.where(classify, my_group, group_map[policy_index])
    logits = lax.dynamic_index_in_dim(logits_all, source, 0, keepdims=False)
    bin_row = lax.dynamic_index_in_dim(bins_all, source, 0, keepdims=False)
    weights_full = group_weights(logits, bin_row, total_len)
    my_shard = lax.axis_index("fsdp")
    weights_local = lax.dynamic_slice_in_dim(weights_full, my_shard * local_rows, local_rows, 0)

    def weight_grad():
        weighted = (weights_full[:, None] * cotangent[0].astype(jnp.float32)).astype(
            jnp.bfloat16
        )
        product = lax.dot_general(
            normed, weighted, (((0,), (0,)), ((), ())), preferred_element_type=jnp.float32
        )
        return (product * total_len ** (-0.5)).astype(jnp.bfloat16)

    def zero_grad():
        return jnp.zeros((normed.shape[1], cotangent.shape[2]), jnp.bfloat16)

    grad = lax.cond(classify, zero_grad, weight_grad)
    return (weights_local[None, :], grad[None])


def solution(mesh):
    in_specs = (
        P("grp", "fsdp", None),
        P("grp", None),
        P("grp", None, "fsdp"),
        P("grp", "fsdp"),
        P("grp", None),
        P("grp", "fsdp"),
        P(),
        P("grp", None, "fsdp"),
    )
    out_specs = (P("grp", "fsdp"), P("grp", None, "fsdp"))
    return jax.shard_map(
        per_device, mesh=mesh, in_specs=in_specs, out_specs=out_specs, check_vma=False
    )
```

```python
import jax
import jax.numpy as jnp
from jax import lax
from jax.sharding import PartitionSpec as P

NBINS = 16


def normalize_rows(rows_in, scale_row):
    values_f = rows_in.astype(jnp.float32)
    mean_sq = jnp.mean(values_f * values_f, axis=-1, keepdims=True)
    return (values_f * lax.rsqrt(mean_sq + 1e-05) * scale_row).astype(jnp.bfloat16)


def segment_ids(length_row, total_len):
    response_ends = jnp.cumsum(length_row)
    positions = jnp.arange(total_len, dtype=jnp.int32)
    return jnp.sum((positions[:, None] >= response_ends[None, :]).astype(jnp.int32), axis=1)


def head_logits(query_rows, key_rows, value_rows, score_row, segment):
    row_count = query_rows.shape[0]
    head_size = query_rows.shape[1]
    scores = jnp.dot(query_rows, key_rows.T, preferred_element_type=jnp.float32) * head_size ** (
        -0.5
    )
    query_pos = jnp.arange(row_count, dtype=jnp.int32)
    key_pos = jnp.arange(key_rows.shape[0], dtype=jnp.int32)
    allowed = (segment[:, None] == segment[None, :]) & (key_pos[None, :] <= query_pos[:, None])
    scores = jnp.where(allowed, scores, -1e30)
    highest = jnp.max(scores, axis=1, keepdims=True)
    expo = jnp.exp(scores - highest)
    weights = (expo / jnp.sum(expo, axis=1, keepdims=True)).astype(jnp.bfloat16)
    mixed = jnp.dot(weights, value_rows, preferred_element_type=jnp.float32)
    return jnp.dot(mixed, score_row, precision=lax.Precision.HIGHEST)


def group_weights(logits, bin_row, total_len):
    onehot = (bin_row[:, None] == jnp.arange(NBINS, dtype=jnp.int32)[None, :]).astype(jnp.float32)
    counts = jnp.sum(onehot, axis=0)
    sums = jnp.dot(jax.nn.sigmoid(logits), onehot, precision=lax.Precision.HIGHEST)
    calib = (counts - sums + 1.0) / (sums + 1.0)
    ratio = jnp.exp(logits) * jnp.dot(onehot, calib, precision=lax.Precision.HIGHEST)
    return ratio * total_len / jnp.sum(ratio)


def per_device(
    layer_input, norm_gain, layer_weight, score_vec, lengths, bins, group_map, cotangent
):
    n_groups = lax.axis_size("grp")
    half_groups = n_groups // 2
    my_group = lax.axis_index("grp")
    classify = my_group < half_groups
    normed = lax.all_gather(
        normalize_rows(layer_input[0], norm_gain[0]), "fsdp", axis=0, tiled=True
    )
    total_len = normed.shape[0]
    head_size = layer_weight.shape[2] // 3
    segment = segment_ids(lengths[0], total_len)
    score_row = score_vec[0].astype(jnp.float32)
    local_rows = bins.shape[1]

    def attend():
        projected = jnp.dot(
            normed, layer_weight[0], preferred_element_type=jnp.float32
        ).astype(jnp.bfloat16)
        return head_logits(
            projected[:, :head_size],
            projected[:, head_size : 2 * head_size],
            projected[:, 2 * head_size :],
            score_row,
            segment,
        )

    def skipped():
        return jnp.zeros((total_len,), jnp.float32)

    contrib = lax.cond(classify, attend, skipped)
    my_shard = lax.axis_index("fsdp")
    n_shards = lax.axis_size("fsdp")
    bins_spread = lax.dynamic_update_slice_in_dim(
        jnp.zeros((total_len,), jnp.float32), bins[0].astype(jnp.float32), my_shard * local_rows, 0
    )
    packed = jnp.stack([contrib, bins_spread])
    step = 1
    while step < n_shards:
        packed = packed + lax.ppermute(
            packed, "fsdp", [(i, i ^ step) for i in range(n_shards)]
        )
        step *= 2
    policy_index = jnp.clip(my_group - half_groups, 0, half_groups - 1)
    source = group_map[policy_index]
    pick = (policy_index - source) % half_groups
    relayed = jnp.zeros_like(packed)
    for shift in range(half_groups):
        moved = lax.ppermute(
            packed,
            "grp",
            [(g, half_groups + (g + shift) % half_groups) for g in range(half_groups)],
        )
        relayed = jnp.where(pick == shift, moved, relayed)
    chosen = jnp.where(classify, packed, relayed)
    logits = chosen[0]
    bin_row = chosen[1].astype(jnp.int32)
    weights_full = group_weights(logits, bin_row, total_len)
    weights_local = lax.dynamic_slice_in_dim(weights_full, my_shard * local_rows, local_rows, 0)

    def weight_grad():
        weighted = (weights_full[:, None] * cotangent[0].astype(jnp.float32)).astype(
            jnp.bfloat16
        )
        product = lax.dot_general(
            normed, weighted, (((0,), (0,)), ((), ())), preferred_element_type=jnp.float32
        )
        return (product * total_len ** (-0.5)).astype(jnp.bfloat16)

    def zero_grad():
        return jnp.zeros((normed.shape[1], cotangent.shape[2]), jnp.bfloat16)

    grad = lax.cond(classify, zero_grad, weight_grad)
    return (weights_local[None, :], grad[None])


def solution(mesh):
    in_specs = (
        P("grp", "fsdp", None),
        P("grp", None),
        P("grp", None, "fsdp"),
        P("grp", "fsdp"),
        P("grp", None),
        P("grp", "fsdp"),
        P(),
        P("grp", None, "fsdp"),
    )
    out_specs = (P("grp", "fsdp"), P("grp", None, "fsdp"))
    return jax.shard_map(
        per_device, mesh=mesh, in_specs=in_specs, out_specs=out_specs, check_vma=False
    )
```

```python
import jax
import jax.numpy as jnp
from jax import lax
from jax.sharding import PartitionSpec as P
from jax.experimental import pallas as pl
from jax.experimental.pallas import tpu as pltpu

NBINS = 16
MAXLEN = 384
PROJ_ROWS = 256


def _project_kernel(rows_ref, weight_ref, out_ref):
    out_ref[...] = jnp.dot(
        rows_ref[...], weight_ref[...], preferred_element_type=jnp.float32
    ).astype(out_ref.dtype)


def project_rows(rows, weight):
    n_rows, depth = rows.shape
    width = weight.shape[1]
    return pl.pallas_call(
        _project_kernel,
        out_shape=jax.ShapeDtypeStruct((n_rows, width), jnp.bfloat16),
        grid=(n_rows // PROJ_ROWS,),
        in_specs=[
            pl.BlockSpec((PROJ_ROWS, depth), lambda i: (i, 0)),
            pl.BlockSpec((depth, width), lambda i: (0, 0)),
        ],
        out_specs=pl.BlockSpec((PROJ_ROWS, width), lambda i: (i, 0)),
        compiler_params=pltpu.CompilerParams(vmem_limit_bytes=48 * 1024 * 1024),
        cost_estimate=pl.CostEstimate(
            flops=2 * n_rows * depth * width,
            bytes_accessed=2 * (n_rows * depth + depth * width + n_rows * width),
            transcendentals=0,
        ),
    )(rows, weight)


def normalize_rows(rows_in, scale_row):
    values_f = rows_in.astype(jnp.float32)
    mean_sq = jnp.mean(values_f * values_f, axis=-1, keepdims=True)
    return (values_f * lax.rsqrt(mean_sq + 1e-05) * scale_row).astype(jnp.bfloat16)


def segment_ids(length_row, total_len):
    response_ends = jnp.cumsum(length_row)
    positions = jnp.arange(total_len, dtype=jnp.int32)
    return jnp.sum((positions[:, None] >= response_ends[None, :]).astype(jnp.int32), axis=1)


def head_logits(query_rows, key_rows, value_rows, score_row, segment):
    row_count, head_size = query_rows.shape
    blocks = row_count // MAXLEN

    def windows(rows, fill):
        padded = jnp.concatenate(
            [jnp.full((MAXLEN,) + rows.shape[1:], fill, rows.dtype), rows], axis=0
        ).reshape((blocks + 1, MAXLEN) + rows.shape[1:])
        return jnp.concatenate([padded[:-1], padded[1:]], axis=1)

    key_win = windows(key_rows, 0)
    value_win = windows(value_rows, 0)
    seg_win = windows(segment, -1)
    pos = jnp.arange(row_count, dtype=jnp.int32)
    pos_win = windows(pos, 0)
    query_blk = query_rows.reshape(blocks, MAXLEN, head_size)
    scores = jnp.einsum(
        "bqd,bkd->bqk", query_blk, key_win, preferred_element_type=jnp.float32
    ) * head_size ** (-0.5)
    seg_q = segment.reshape(blocks, MAXLEN)
    pos_q = pos.reshape(blocks, MAXLEN)
    allowed = (seg_q[:, :, None] == seg_win[:, None, :]) & (
        pos_win[:, None, :] <= pos_q[:, :, None]
    )
    scores = jnp.where(allowed, scores, -1e30)
    highest = jnp.max(scores, axis=2, keepdims=True)
    expo = jnp.exp(scores - highest)
    weights = (expo / jnp.sum(expo, axis=2, keepdims=True)).astype(jnp.bfloat16)
    mixed = jnp.einsum("bqk,bkd->bqd", weights, value_win, preferred_element_type=jnp.float32)
    return jnp.dot(
        mixed.reshape(row_count, head_size), score_row, precision=lax.Precision.HIGHEST
    )


def group_weights(logits, bin_row, total_len):
    onehot = (bin_row[:, None] == jnp.arange(NBINS, dtype=jnp.int32)[None, :]).astype(jnp.float32)
    counts = jnp.sum(onehot, axis=0)
    sums = jnp.dot(jax.nn.sigmoid(logits), onehot, precision=lax.Precision.HIGHEST)
    calib = (counts - sums + 1.0) / (sums + 1.0)
    ratio = jnp.exp(logits) * jnp.dot(onehot, calib, precision=lax.Precision.HIGHEST)
    return ratio * total_len / jnp.sum(ratio)


def per_device(
    layer_input, norm_gain, layer_weight, score_vec, lengths, bins, group_map, cotangent
):
    n_groups = lax.axis_size("grp")
    half_groups = n_groups // 2
    my_group = lax.axis_index("grp")
    classify = my_group < half_groups
    normed = lax.all_gather(
        normalize_rows(layer_input[0], norm_gain[0]), "fsdp", axis=0, tiled=True
    )
    total_len = normed.shape[0]
    head_size = layer_weight.shape[2] // 3
    segment = segment_ids(lengths[0], total_len)
    score_row = score_vec[0].astype(jnp.float32)
    local_rows = bins.shape[1]

    def attend():
        projected = project_rows(normed, layer_weight[0])
        return head_logits(
            projected[:, :head_size],
            projected[:, head_size : 2 * head_size],
            projected[:, 2 * head_size :],
            score_row,
            segment,
        )

    def skipped():
        return jnp.zeros((total_len,), jnp.float32)

    contrib = lax.cond(classify, attend, skipped)
    my_shard = lax.axis_index("fsdp")
    n_shards = lax.axis_size("fsdp")
    bins_spread = lax.dynamic_update_slice_in_dim(
        jnp.zeros((total_len,), jnp.float32), bins[0].astype(jnp.float32), my_shard * local_rows, 0
    )
    packed = jnp.stack([contrib, bins_spread])
    step = 1
    while step < n_shards:
        packed = packed + lax.ppermute(
            packed, "fsdp", [(i, i ^ step) for i in range(n_shards)]
        )
        step *= 2
    policy_index = jnp.clip(my_group - half_groups, 0, half_groups - 1)
    source = group_map[policy_index]
    pick = (policy_index - source) % half_groups
    relayed = jnp.zeros_like(packed)
    for shift in range(half_groups):
        moved = lax.ppermute(
            packed,
            "grp",
            [(g, half_groups + (g + shift) % half_groups) for g in range(half_groups)],
        )
        relayed = jnp.where(pick == shift, moved, relayed)
    chosen = jnp.where(classify, packed, relayed)
    logits = chosen[0]
    bin_row = chosen[1].astype(jnp.int32)
    weights_full = group_weights(logits, bin_row, total_len)
    weights_local = lax.dynamic_slice_in_dim(weights_full, my_shard * local_rows, local_rows, 0)

    def weight_grad():
        weighted = (weights_full[:, None] * cotangent[0].astype(jnp.float32)).astype(
            jnp.bfloat16
        )
        product = lax.dot_general(
            normed, weighted, (((0,), (0,)), ((), ())), preferred_element_type=jnp.float32
        )
        return (product * total_len ** (-0.5)).astype(jnp.bfloat16)

    def zero_grad():
        return jnp.zeros((normed.shape[1], cotangent.shape[2]), jnp.bfloat16)

    grad = lax.cond(classify, zero_grad, weight_grad)
    return (weights_local[None, :], grad[None])


def solution(mesh):
    in_specs = (
        P("grp", "fsdp", None),
        P("grp", None),
        P("grp", None, "fsdp"),
        P("grp", "fsdp"),
        P("grp", None),
        P("grp", "fsdp"),
        P(),
        P("grp", None, "fsdp"),
    )
    out_specs = (P("grp", "fsdp"), P("grp", None, "fsdp"))
    return jax.shard_map(
        per_device, mesh=mesh, in_specs=in_specs, out_specs=out_specs, check_vma=False
    )
```

```python
import jax
import jax.numpy as jnp
from jax import lax
from jax.sharding import PartitionSpec as P
from jax.experimental import pallas as pl
from jax.experimental.pallas import tpu as pltpu

NBINS = 16
MAXLEN = 384
PROJ_ROWS = 256


def _project_kernel(rows_ref, weight_ref, out_ref):
    out_ref[...] = jnp.dot(
        rows_ref[...], weight_ref[...], preferred_element_type=jnp.float32
    ).astype(out_ref.dtype)


def project_rows(rows, weight):
    n_rows, depth = rows.shape
    width = weight.shape[1]
    return pl.pallas_call(
        _project_kernel,
        out_shape=jax.ShapeDtypeStruct((n_rows, width), jnp.bfloat16),
        grid=(n_rows // PROJ_ROWS,),
        in_specs=[
            pl.BlockSpec((PROJ_ROWS, depth), lambda i: (i, 0)),
            pl.BlockSpec((depth, width), lambda i: (0, 0)),
        ],
        out_specs=pl.BlockSpec((PROJ_ROWS, width), lambda i: (i, 0)),
        compiler_params=pltpu.CompilerParams(vmem_limit_bytes=48 * 1024 * 1024),
        cost_estimate=pl.CostEstimate(
            flops=2 * n_rows * depth * width,
            bytes_accessed=2 * (n_rows * depth + depth * width + n_rows * width),
            transcendentals=0,
        ),
    )(rows, weight)


def normalize_rows(rows_in, scale_row):
    values_f = rows_in.astype(jnp.float32)
    mean_sq = jnp.mean(values_f * values_f, axis=-1, keepdims=True)
    return (values_f * lax.rsqrt(mean_sq + 1e-05) * scale_row).astype(jnp.bfloat16)


def segment_ids(length_row, total_len):
    response_ends = jnp.cumsum(length_row)
    positions = jnp.arange(total_len, dtype=jnp.int32)
    return jnp.sum((positions[:, None] >= response_ends[None, :]).astype(jnp.int32), axis=1)


def head_logits(query_rows, key_rows, value_rows, score_row, segment):
    row_count, head_size = query_rows.shape
    blocks = row_count // MAXLEN

    def windows(rows, fill):
        padded = jnp.concatenate(
            [jnp.full((MAXLEN,) + rows.shape[1:], fill, rows.dtype), rows], axis=0
        ).reshape((blocks + 1, MAXLEN) + rows.shape[1:])
        return jnp.concatenate([padded[:-1], padded[1:]], axis=1)

    key_win = windows(key_rows, 0)
    value_win = windows(value_rows, 0)
    seg_win = windows(segment, -1)
    pos = jnp.arange(row_count, dtype=jnp.int32)
    pos_win = windows(pos, 0)
    query_blk = query_rows.reshape(blocks, MAXLEN, head_size)
    scores = jnp.einsum(
        "bqd,bkd->bqk", query_blk, key_win, preferred_element_type=jnp.float32
    ) * head_size ** (-0.5)
    seg_q = segment.reshape(blocks, MAXLEN)
    pos_q = pos.reshape(blocks, MAXLEN)
    allowed = (seg_q[:, :, None] == seg_win[:, None, :]) & (
        pos_win[:, None, :] <= pos_q[:, :, None]
    )
    scores = jnp.where(allowed, scores, -1e30)
    highest = jnp.max(scores, axis=2, keepdims=True)
    expo = jnp.exp(scores - highest)
    weights = (expo / jnp.sum(expo, axis=2, keepdims=True)).astype(jnp.bfloat16)
    mixed = jnp.einsum("bqk,bkd->bqd", weights, value_win, preferred_element_type=jnp.float32)
    return jnp.dot(
        mixed.reshape(row_count, head_size), score_row, precision=lax.Precision.HIGHEST
    )


GRAD_COLS = 1024


def _grad_kernel(scale, weighted_t_ref, rows_ref, out_ref):
    product = jnp.dot(weighted_t_ref[...], rows_ref[...], preferred_element_type=jnp.float32)
    out_ref[...] = (product * scale).T.astype(out_ref.dtype)


def weight_grad_rows(rows, weighted_t, scale):
    n_rows, depth = rows.shape
    width = weighted_t.shape[0]
    return pl.pallas_call(
        lambda *refs: _grad_kernel(scale, *refs),
        out_shape=jax.ShapeDtypeStruct((depth, width), jnp.bfloat16),
        grid=(depth // GRAD_COLS,),
        in_specs=[
            pl.BlockSpec((width, n_rows), lambda i: (0, 0)),
            pl.BlockSpec((n_rows, GRAD_COLS), lambda i: (0, i)),
        ],
        out_specs=pl.BlockSpec((GRAD_COLS, width), lambda i: (i, 0)),
        compiler_params=pltpu.CompilerParams(vmem_limit_bytes=48 * 1024 * 1024),
        cost_estimate=pl.CostEstimate(
            flops=2 * n_rows * depth * width,
            bytes_accessed=2 * (n_rows * depth + n_rows * width + depth * width),
            transcendentals=0,
        ),
    )(weighted_t, rows)


def group_weights(logits, bin_row, total_len):
    onehot = (bin_row[:, None] == jnp.arange(NBINS, dtype=jnp.int32)[None, :]).astype(jnp.float32)
    counts = jnp.sum(onehot, axis=0)
    sums = jnp.dot(jax.nn.sigmoid(logits), onehot, precision=lax.Precision.HIGHEST)
    calib = (counts - sums + 1.0) / (sums + 1.0)
    ratio = jnp.exp(logits) * jnp.dot(onehot, calib, precision=lax.Precision.HIGHEST)
    return ratio * total_len / jnp.sum(ratio)


def per_device(
    layer_input, norm_gain, layer_weight, score_vec, lengths, bins, group_map, cotangent
):
    n_groups = lax.axis_size("grp")
    half_groups = n_groups // 2
    my_group = lax.axis_index("grp")
    classify = my_group < half_groups
    normed = lax.all_gather(
        normalize_rows(layer_input[0], norm_gain[0]), "fsdp", axis=0, tiled=True
    )
    total_len = normed.shape[0]
    head_size = layer_weight.shape[2] // 3
    segment = segment_ids(lengths[0], total_len)
    score_row = score_vec[0].astype(jnp.float32)
    local_rows = bins.shape[1]

    def attend():
        projected = project_rows(normed, layer_weight[0])
        return head_logits(
            projected[:, :head_size],
            projected[:, head_size : 2 * head_size],
            projected[:, 2 * head_size :],
            score_row,
            segment,
        )

    def skipped():
        return jnp.zeros((total_len,), jnp.float32)

    contrib = lax.cond(classify, attend, skipped)
    my_shard = lax.axis_index("fsdp")
    n_shards = lax.axis_size("fsdp")
    bins_spread = lax.dynamic_update_slice_in_dim(
        jnp.zeros((total_len,), jnp.float32), bins[0].astype(jnp.float32), my_shard * local_rows, 0
    )
    packed = jnp.stack([contrib, bins_spread])
    step = 1
    while step < n_shards // 2:
        packed = packed + lax.ppermute(
            packed, "fsdp", [(i, i ^ step) for i in range(n_shards)]
        )
        step *= 2
    half_sum = packed
    packed = half_sum + lax.ppermute(half_sum, "fsdp", [(i, i ^ step) for i in range(n_shards)])
    policy_index = jnp.clip(my_group - half_groups, 0, half_groups - 1)
    source = group_map[policy_index]
    pick = (policy_index - source) % half_groups
    relayed = jnp.zeros_like(packed)
    for shift in range(half_groups):
        parts = []
        for flip in (0, step):
            parts.append(
                lax.ppermute(
                    half_sum,
                    ("grp", "fsdp"),
                    [
                        (g * n_shards + i, (half_groups + (g + shift) % half_groups) * n_shards + (i ^ flip))
                        for g in range(half_groups)
                        for i in range(n_shards)
                    ],
                )
            )
        relayed = jnp.where(pick == shift, parts[0] + parts[1], relayed)
    chosen = jnp.where(classify, packed, relayed)
    logits = chosen[0]
    bin_row = chosen[1].astype(jnp.int32)
    weights_full = group_weights(logits, bin_row, total_len)
    weights_local = lax.dynamic_slice_in_dim(weights_full, my_shard * local_rows, local_rows, 0)

    def weight_grad():
        weighted = (weights_full[:, None] * cotangent[0].astype(jnp.float32)).astype(
            jnp.bfloat16
        )
        return weight_grad_rows(normed, weighted.T, total_len ** (-0.5))

    def zero_grad():
        return jnp.zeros((normed.shape[1], cotangent.shape[2]), jnp.bfloat16)

    grad = lax.cond(classify, zero_grad, weight_grad)
    return (weights_local[None, :], grad[None])


def solution(mesh):
    in_specs = (
        P("grp", "fsdp", None),
        P("grp", None),
        P("grp", None, "fsdp"),
        P("grp", "fsdp"),
        P("grp", None),
        P("grp", "fsdp"),
        P(),
        P("grp", None, "fsdp"),
    )
    out_specs = (P("grp", "fsdp"), P("grp", None, "fsdp"))
    return jax.shard_map(
        per_device, mesh=mesh, in_specs=in_specs, out_specs=out_specs, check_vma=False
    )
```

```python
import jax
import jax.numpy as jnp
from jax import lax
from jax.sharding import PartitionSpec as P
from jax.experimental import pallas as pl
from jax.experimental.pallas import tpu as pltpu

NBINS = 16
PROJ_ROWS = 256


def _project_kernel(rows_ref, weight_ref, out_ref):
    out_ref[...] = jnp.dot(
        rows_ref[...], weight_ref[...], preferred_element_type=jnp.float32
    ).astype(out_ref.dtype)


def project_rows(rows, weight):
    n_rows, depth = rows.shape
    width = weight.shape[1]
    return pl.pallas_call(
        _project_kernel,
        out_shape=jax.ShapeDtypeStruct((n_rows, width), jnp.bfloat16),
        grid=(n_rows // PROJ_ROWS,),
        in_specs=[
            pl.BlockSpec((PROJ_ROWS, depth), lambda i: (i, 0)),
            pl.BlockSpec((depth, width), lambda i: (0, 0)),
        ],
        out_specs=pl.BlockSpec((PROJ_ROWS, width), lambda i: (i, 0)),
        compiler_params=pltpu.CompilerParams(vmem_limit_bytes=48 * 1024 * 1024),
        cost_estimate=pl.CostEstimate(
            flops=2 * n_rows * depth * width,
            bytes_accessed=2 * (n_rows * depth + depth * width + n_rows * width),
            transcendentals=0,
        ),
    )(rows, weight)


def normalize_rows(rows_in, scale_row):
    values_f = rows_in.astype(jnp.float32)
    mean_sq = jnp.mean(values_f * values_f, axis=-1, keepdims=True)
    return (values_f * lax.rsqrt(mean_sq + 1e-05) * scale_row).astype(jnp.bfloat16)


def segment_ids(length_row, total_len):
    response_ends = jnp.cumsum(length_row)
    positions = jnp.arange(total_len, dtype=jnp.int32)
    return jnp.sum((positions[:, None] >= response_ends[None, :]).astype(jnp.int32), axis=1)


def head_logits(query_rows, key_rows, value_rows, score_row, segment):
    row_count = query_rows.shape[0]
    head_size = query_rows.shape[1]
    scores = jnp.dot(query_rows, key_rows.T, preferred_element_type=jnp.float32) * head_size ** (
        -0.5
    )
    query_pos = jnp.arange(row_count, dtype=jnp.int32)
    key_pos = jnp.arange(key_rows.shape[0], dtype=jnp.int32)
    allowed = (segment[:, None] == segment[None, :]) & (key_pos[None, :] <= query_pos[:, None])
    scores = jnp.where(allowed, scores, -1e30)
    highest = jnp.max(scores, axis=1, keepdims=True)
    expo = jnp.exp(scores - highest)
    weights = (expo / jnp.sum(expo, axis=1, keepdims=True)).astype(jnp.bfloat16)
    mixed = jnp.dot(weights, value_rows, preferred_element_type=jnp.float32)
    return jnp.dot(mixed, score_row, precision=lax.Precision.HIGHEST)


GRAD_COLS = 1024


def _grad_kernel(scale, weighted_t_ref, rows_ref, out_ref):
    product = jnp.dot(weighted_t_ref[...], rows_ref[...], preferred_element_type=jnp.float32)
    out_ref[...] = (product * scale).T.astype(out_ref.dtype)


def weight_grad_rows(rows, weighted_t, scale):
    n_rows, depth = rows.shape
    width = weighted_t.shape[0]
    return pl.pallas_call(
        lambda *refs: _grad_kernel(scale, *refs),
        out_shape=jax.ShapeDtypeStruct((depth, width), jnp.bfloat16),
        grid=(depth // GRAD_COLS,),
        in_specs=[
            pl.BlockSpec((width, n_rows), lambda i: (0, 0)),
            pl.BlockSpec((n_rows, GRAD_COLS), lambda i: (0, i)),
        ],
        out_specs=pl.BlockSpec((GRAD_COLS, width), lambda i: (i, 0)),
        compiler_params=pltpu.CompilerParams(vmem_limit_bytes=48 * 1024 * 1024),
        cost_estimate=pl.CostEstimate(
            flops=2 * n_rows * depth * width,
            bytes_accessed=2 * (n_rows * depth + n_rows * width + depth * width),
            transcendentals=0,
        ),
    )(weighted_t, rows)


def group_weights(logits, bin_row, total_len):
    onehot = (bin_row[:, None] == jnp.arange(NBINS, dtype=jnp.int32)[None, :]).astype(jnp.float32)
    counts = jnp.sum(onehot, axis=0)
    sums = jnp.dot(jax.nn.sigmoid(logits), onehot, precision=lax.Precision.HIGHEST)
    calib = (counts - sums + 1.0) / (sums + 1.0)
    ratio = jnp.exp(logits) * jnp.dot(onehot, calib, precision=lax.Precision.HIGHEST)
    return ratio * total_len / jnp.sum(ratio)


def per_device(
    layer_input, norm_gain, layer_weight, score_vec, lengths, bins, group_map, cotangent
):
    n_groups = lax.axis_size("grp")
    half_groups = n_groups // 2
    my_group = lax.axis_index("grp")
    classify = my_group < half_groups
    normed = lax.all_gather(
        normalize_rows(layer_input[0], norm_gain[0]), "fsdp", axis=0, tiled=True
    )
    total_len = normed.shape[0]
    head_size = layer_weight.shape[2] // 3
    segment = segment_ids(lengths[0], total_len)
    score_row = score_vec[0].astype(jnp.float32)
    local_rows = bins.shape[1]

    def attend():
        projected = project_rows(normed, layer_weight[0])
        return head_logits(
            projected[:, :head_size],
            projected[:, head_size : 2 * head_size],
            projected[:, 2 * head_size :],
            score_row,
            segment,
        )

    def skipped():
        return jnp.zeros((total_len,), jnp.float32)

    contrib = lax.cond(classify, attend, skipped)
    my_shard = lax.axis_index("fsdp")
    n_shards = lax.axis_size("fsdp")
    bins_spread = lax.dynamic_update_slice_in_dim(
        jnp.zeros((total_len,), jnp.float32), bins[0].astype(jnp.float32), my_shard * local_rows, 0
    )
    packed = jnp.stack([contrib, bins_spread])
    step = 1
    while step < n_shards // 2:
        packed = packed + lax.ppermute(
            packed, "fsdp", [(i, i ^ step) for i in range(n_shards)]
        )
        step *= 2
    half_sum = packed
    packed = half_sum + lax.ppermute(half_sum, "fsdp", [(i, i ^ step) for i in range(n_shards)])
    policy_index = jnp.clip(my_group - half_groups, 0, half_groups - 1)
    source = group_map[policy_index]
    pick = (policy_index - source) % half_groups
    relayed = jnp.zeros_like(packed)
    for shift in range(half_groups):
        parts = []
        for flip in (0, step):
            parts.append(
                lax.ppermute(
                    half_sum,
                    ("grp", "fsdp"),
                    [
                        (g * n_shards + i, (half_groups + (g + shift) % half_groups) * n_shards + (i ^ flip))
                        for g in range(half_groups)
                        for i in range(n_shards)
                    ],
                )
            )
        relayed = jnp.where(pick == shift, parts[0] + parts[1], relayed)
    chosen = jnp.where(classify, packed, relayed)
    logits = chosen[0]
    bin_row = chosen[1].astype(jnp.int32)
    weights_full = group_weights(logits, bin_row, total_len)
    weights_local = lax.dynamic_slice_in_dim(weights_full, my_shard * local_rows, local_rows, 0)

    def weight_grad():
        weighted = (weights_full[:, None] * cotangent[0].astype(jnp.float32)).astype(
            jnp.bfloat16
        )
        return weight_grad_rows(normed, weighted.T, total_len ** (-0.5))

    def zero_grad():
        return jnp.zeros((normed.shape[1], cotangent.shape[2]), jnp.bfloat16)

    grad = lax.cond(classify, zero_grad, weight_grad)
    return (weights_local[None, :], grad[None])


def solution(mesh):
    in_specs = (
        P("grp", "fsdp", None),
        P("grp", None),
        P("grp", None, "fsdp"),
        P("grp", "fsdp"),
        P("grp", None),
        P("grp", "fsdp"),
        P(),
        P("grp", None, "fsdp"),
    )
    out_specs = (P("grp", "fsdp"), P("grp", None, "fsdp"))
    return jax.shard_map(
        per_device, mesh=mesh, in_specs=in_specs, out_specs=out_specs, check_vma=False
    )
```

```python
import jax
import jax.numpy as jnp
from jax import lax
from jax.sharding import PartitionSpec as P
from jax.experimental import pallas as pl
from jax.experimental.pallas import tpu as pltpu

NBINS = 16
PROJ_ROWS = 256


def _project_kernel(rows_ref, weight_ref, out_ref):
    out_ref[...] = jnp.dot(
        rows_ref[...], weight_ref[...], preferred_element_type=jnp.float32
    ).astype(out_ref.dtype)


def project_rows(rows, weight):
    n_rows, depth = rows.shape
    width = weight.shape[1]
    return pl.pallas_call(
        _project_kernel,
        out_shape=jax.ShapeDtypeStruct((n_rows, width), jnp.bfloat16),
        grid=(n_rows // PROJ_ROWS,),
        in_specs=[
            pl.BlockSpec((PROJ_ROWS, depth), lambda i: (i, 0)),
            pl.BlockSpec((depth, width), lambda i: (0, 0)),
        ],
        out_specs=pl.BlockSpec((PROJ_ROWS, width), lambda i: (i, 0)),
        compiler_params=pltpu.CompilerParams(vmem_limit_bytes=48 * 1024 * 1024),
        cost_estimate=pl.CostEstimate(
            flops=2 * n_rows * depth * width,
            bytes_accessed=2 * (n_rows * depth + depth * width + n_rows * width),
            transcendentals=0,
        ),
    )(rows, weight)


def _normalize_kernel(rows_ref, scale_ref, out_ref):
    values_f = rows_ref[...].astype(jnp.float32)
    mean_sq = jnp.mean(values_f * values_f, axis=-1, keepdims=True)
    out_ref[...] = (values_f * lax.rsqrt(mean_sq + 1e-05) * scale_ref[...]).astype(out_ref.dtype)


def normalize_rows(rows_in, scale_row):
    return pl.pallas_call(
        _normalize_kernel,
        out_shape=jax.ShapeDtypeStruct(rows_in.shape, jnp.bfloat16),
        cost_estimate=pl.CostEstimate(
            flops=4 * rows_in.size, bytes_accessed=4 * rows_in.size, transcendentals=rows_in.shape[0]
        ),
    )(rows_in, scale_row[None, :])


def segment_ids(length_row, total_len):
    response_ends = jnp.cumsum(length_row)
    positions = jnp.arange(total_len, dtype=jnp.int32)
    return jnp.sum((positions[:, None] >= response_ends[None, :]).astype(jnp.int32), axis=1)


def head_logits(query_rows, key_rows, value_rows, score_row, segment):
    row_count = query_rows.shape[0]
    head_size = query_rows.shape[1]
    scores = jnp.dot(query_rows, key_rows.T, preferred_element_type=jnp.float32) * head_size ** (
        -0.5
    )
    query_pos = jnp.arange(row_count, dtype=jnp.int32)
    key_pos = jnp.arange(key_rows.shape[0], dtype=jnp.int32)
    allowed = (segment[:, None] == segment[None, :]) & (key_pos[None, :] <= query_pos[:, None])
    scores = jnp.where(allowed, scores, -1e30)
    highest = jnp.max(scores, axis=1, keepdims=True)
    expo = jnp.exp(scores - highest)
    weights = (expo / jnp.sum(expo, axis=1, keepdims=True)).astype(jnp.bfloat16)
    mixed = jnp.dot(weights, value_rows, preferred_element_type=jnp.float32)
    return jnp.dot(mixed, score_row, precision=lax.Precision.HIGHEST)


GRAD_COLS = 1024


def _grad_kernel(scale, weighted_t_ref, rows_ref, out_ref):
    product = jnp.dot(weighted_t_ref[...], rows_ref[...], preferred_element_type=jnp.float32)
    out_ref[...] = (product * scale).T.astype(out_ref.dtype)


def weight_grad_rows(rows, weighted_t, scale):
    n_rows, depth = rows.shape
    width = weighted_t.shape[0]
    return pl.pallas_call(
        lambda *refs: _grad_kernel(scale, *refs),
        out_shape=jax.ShapeDtypeStruct((depth, width), jnp.bfloat16),
        grid=(depth // GRAD_COLS,),
        in_specs=[
            pl.BlockSpec((width, n_rows), lambda i: (0, 0)),
            pl.BlockSpec((n_rows, GRAD_COLS), lambda i: (0, i)),
        ],
        out_specs=pl.BlockSpec((GRAD_COLS, width), lambda i: (i, 0)),
        compiler_params=pltpu.CompilerParams(vmem_limit_bytes=48 * 1024 * 1024),
        cost_estimate=pl.CostEstimate(
            flops=2 * n_rows * depth * width,
            bytes_accessed=2 * (n_rows * depth + n_rows * width + depth * width),
            transcendentals=0,
        ),
    )(weighted_t, rows)


def group_weights(logits, bin_row, total_len):
    onehot = (bin_row[:, None] == jnp.arange(NBINS, dtype=jnp.int32)[None, :]).astype(jnp.float32)
    counts = jnp.sum(onehot, axis=0)
    sums = jnp.dot(jax.nn.sigmoid(logits), onehot, precision=lax.Precision.HIGHEST)
    calib = (counts - sums + 1.0) / (sums + 1.0)
    ratio = jnp.exp(logits) * jnp.dot(onehot, calib, precision=lax.Precision.HIGHEST)
    return ratio * total_len / jnp.sum(ratio)


def per_device(
    layer_input, norm_gain, layer_weight, score_vec, lengths, bins, group_map, cotangent
):
    n_groups = lax.axis_size("grp")
    half_groups = n_groups // 2
    my_group = lax.axis_index("grp")
    classify = my_group < half_groups
    normed = lax.all_gather(
        normalize_rows(layer_input[0], norm_gain[0]), "fsdp", axis=0, tiled=True
    )
    total_len = normed.shape[0]
    head_size = layer_weight.shape[2] // 3
    segment = segment_ids(lengths[0], total_len)
    score_row = score_vec[0].astype(jnp.float32)
    local_rows = bins.shape[1]

    def attend():
        projected = project_rows(normed, layer_weight[0])
        return head_logits(
            projected[:, :head_size],
            projected[:, head_size : 2 * head_size],
            projected[:, 2 * head_size :],
            score_row,
            segment,
        )

    def skipped():
        return jnp.zeros((total_len,), jnp.float32)

    contrib = lax.cond(classify, attend, skipped)
    my_shard = lax.axis_index("fsdp")
    n_shards = lax.axis_size("fsdp")
    bins_spread = lax.dynamic_update_slice_in_dim(
        jnp.zeros((total_len,), jnp.float32), bins[0].astype(jnp.float32), my_shard * local_rows, 0
    )
    packed = jnp.stack([contrib, bins_spread])
    step = 1
    while step < n_shards:
        packed = packed + lax.ppermute(
            packed, "fsdp", [(i, i ^ step) for i in range(n_shards)]
        )
        step *= 2
    policy_index = jnp.clip(my_group - half_groups, 0, half_groups - 1)
    source = group_map[policy_index]
    pick = (policy_index - source) % half_groups
    relayed = jnp.zeros_like(packed)
    for shift in range(half_groups):
        moved = lax.ppermute(
            packed,
            "grp",
            [(g, half_groups + (g + shift) % half_groups) for g in range(half_groups)],
        )
        relayed = jnp.where(pick == shift, moved, relayed)
    chosen = jnp.where(classify, packed, relayed)
    logits = chosen[0]
    bin_row = chosen[1].astype(jnp.int32)
    weights_full = group_weights(logits, bin_row, total_len)
    weights_local = lax.dynamic_slice_in_dim(weights_full, my_shard * local_rows, local_rows, 0)

    def weight_grad():
        weighted = (weights_full[:, None] * cotangent[0].astype(jnp.float32)).astype(
            jnp.bfloat16
        )
        return weight_grad_rows(normed, weighted.T, total_len ** (-0.5))

    def zero_grad():
        return jnp.zeros((normed.shape[1], cotangent.shape[2]), jnp.bfloat16)

    grad = lax.cond(classify, zero_grad, weight_grad)
    return (weights_local[None, :], grad[None])


def solution(mesh):
    in_specs = (
        P("grp", "fsdp", None),
        P("grp", None),
        P("grp", None, "fsdp"),
        P("grp", "fsdp"),
        P("grp", None),
        P("grp", "fsdp"),
        P(),
        P("grp", None, "fsdp"),
    )
    out_specs = (P("grp", "fsdp"), P("grp", None, "fsdp"))
    return jax.shard_map(
        per_device, mesh=mesh, in_specs=in_specs, out_specs=out_specs, check_vma=False
    )
```

```python
import jax
import jax.numpy as jnp
from jax import lax
from jax.sharding import PartitionSpec as P
from jax.experimental import pallas as pl
from jax.experimental.pallas import tpu as pltpu

NBINS = 16
PROJ_ROWS = 256


def _project_kernel(rows_ref, weight_ref, out_ref):
    out_ref[...] = jnp.dot(
        rows_ref[...], weight_ref[...], preferred_element_type=jnp.float32
    ).astype(out_ref.dtype)


def project_rows(rows, weight):
    n_rows, depth = rows.shape
    width = weight.shape[1]
    return pl.pallas_call(
        _project_kernel,
        out_shape=jax.ShapeDtypeStruct((n_rows, width), jnp.bfloat16),
        grid=(n_rows // PROJ_ROWS,),
        in_specs=[
            pl.BlockSpec((PROJ_ROWS, depth), lambda i: (i, 0)),
            pl.BlockSpec((depth, width), lambda i: (0, 0)),
        ],
        out_specs=pl.BlockSpec((PROJ_ROWS, width), lambda i: (i, 0)),
        compiler_params=pltpu.CompilerParams(vmem_limit_bytes=48 * 1024 * 1024),
        cost_estimate=pl.CostEstimate(
            flops=2 * n_rows * depth * width,
            bytes_accessed=2 * (n_rows * depth + depth * width + n_rows * width),
            transcendentals=0,
        ),
    )(rows, weight)


def _normalize_kernel(rows_ref, scale_ref, out_ref):
    values_f = rows_ref[...].astype(jnp.float32)
    mean_sq = jnp.mean(values_f * values_f, axis=-1, keepdims=True)
    out_ref[...] = (values_f * lax.rsqrt(mean_sq + 1e-05) * scale_ref[...]).astype(out_ref.dtype)


def normalize_rows(rows_in, scale_row):
    return pl.pallas_call(
        _normalize_kernel,
        out_shape=jax.ShapeDtypeStruct(rows_in.shape, jnp.bfloat16),
        cost_estimate=pl.CostEstimate(
            flops=4 * rows_in.size, bytes_accessed=4 * rows_in.size, transcendentals=rows_in.shape[0]
        ),
    )(rows_in, scale_row[None, :])


def segment_ids(length_row, total_len):
    response_ends = jnp.cumsum(length_row)
    positions = jnp.arange(total_len, dtype=jnp.int32)
    return jnp.sum((positions[:, None] >= response_ends[None, :]).astype(jnp.int32), axis=1)


def head_logits(query_rows, key_rows, value_rows, score_row, segment):
    row_count = query_rows.shape[0]
    head_size = query_rows.shape[1]
    scores = jnp.dot(query_rows, key_rows.T, preferred_element_type=jnp.float32) * head_size ** (
        -0.5
    )
    query_pos = jnp.arange(row_count, dtype=jnp.int32)
    key_pos = jnp.arange(key_rows.shape[0], dtype=jnp.int32)
    allowed = (segment[:, None] == segment[None, :]) & (key_pos[None, :] <= query_pos[:, None])
    scores = jnp.where(allowed, scores, -1e30)
    highest = jnp.max(scores, axis=1, keepdims=True)
    expo = jnp.exp(scores - highest)
    weights = (expo / jnp.sum(expo, axis=1, keepdims=True)).astype(jnp.bfloat16)
    mixed = jnp.dot(weights, value_rows, preferred_element_type=jnp.float32)
    return jnp.dot(mixed, score_row, precision=lax.Precision.HIGHEST)


GRAD_COLS = 1024


def _grad_kernel(scale, weighted_t_ref, rows_ref, out_ref):
    product = jnp.dot(weighted_t_ref[...], rows_ref[...], preferred_element_type=jnp.float32)
    out_ref[...] = (product * scale).T.astype(out_ref.dtype)


def weight_grad_rows(rows, weighted_t, scale):
    n_rows, depth = rows.shape
    width = weighted_t.shape[0]
    return pl.pallas_call(
        lambda *refs: _grad_kernel(scale, *refs),
        out_shape=jax.ShapeDtypeStruct((depth, width), jnp.bfloat16),
        grid=(depth // GRAD_COLS,),
        in_specs=[
            pl.BlockSpec((width, n_rows), lambda i: (0, 0)),
            pl.BlockSpec((n_rows, GRAD_COLS), lambda i: (0, i)),
        ],
        out_specs=pl.BlockSpec((GRAD_COLS, width), lambda i: (i, 0)),
        compiler_params=pltpu.CompilerParams(vmem_limit_bytes=48 * 1024 * 1024),
        cost_estimate=pl.CostEstimate(
            flops=2 * n_rows * depth * width,
            bytes_accessed=2 * (n_rows * depth + n_rows * width + depth * width),
            transcendentals=0,
        ),
    )(weighted_t, rows)


def group_weights(logits, bin_row, total_len):
    onehot = (bin_row[:, None] == jnp.arange(NBINS, dtype=jnp.int32)[None, :]).astype(jnp.float32)
    counts = jnp.sum(onehot, axis=0)
    sums = jnp.dot(jax.nn.sigmoid(logits), onehot, precision=lax.Precision.HIGHEST)
    calib = (counts - sums + 1.0) / (sums + 1.0)
    ratio = jnp.exp(logits) * jnp.dot(onehot, calib, precision=lax.Precision.HIGHEST)
    return ratio * total_len / jnp.sum(ratio)


def per_device(
    layer_input, norm_gain, layer_weight, score_vec, lengths, bins, group_map, cotangent
):
    n_groups = lax.axis_size("grp")
    half_groups = n_groups // 2
    my_group = lax.axis_index("grp")
    classify = my_group < half_groups
    normed = lax.all_gather(
        normalize_rows(layer_input[0], norm_gain[0]), "fsdp", axis=0, tiled=True
    )
    total_len = normed.shape[0]
    head_size = layer_weight.shape[2] // 3
    segment = segment_ids(lengths[0], total_len)
    score_row = score_vec[0].astype(jnp.float32)
    local_rows = bins.shape[1]

    def attend():
        projected = project_rows(normed, layer_weight[0])
        return head_logits(
            projected[:, :head_size],
            projected[:, head_size : 2 * head_size],
            projected[:, 2 * head_size :],
            score_row,
            segment,
        )

    def skipped():
        return jnp.zeros((total_len,), jnp.float32)

    contrib = lax.cond(classify, attend, skipped)
    my_shard = lax.axis_index("fsdp")
    n_shards = lax.axis_size("fsdp")
    bins_spread = lax.dynamic_update_slice_in_dim(
        jnp.zeros((total_len,), jnp.float32), bins[0].astype(jnp.float32), my_shard * local_rows, 0
    )
    packed = jnp.stack([contrib, bins_spread])
    step = 1
    while step < n_shards:
        packed = packed + lax.ppermute(
            packed, "fsdp", [(i, i ^ step) for i in range(n_shards)]
        )
        step *= 2
    policy_index = jnp.clip(my_group - half_groups, 0, half_groups - 1)
    source = group_map[policy_index]
    pick = (policy_index - source) % half_groups
    relayed = jnp.zeros_like(packed)
    for shift in range(half_groups):
        moved = lax.ppermute(
            packed,
            "grp",
            [(g, half_groups + (g + shift) % half_groups) for g in range(half_groups)],
        )
        relayed = jnp.where(pick == shift, moved, relayed)
    chosen = jnp.where(classify, packed, relayed)
    logits = chosen[0]
    bin_row = chosen[1].astype(jnp.int32)
    weights_full = group_weights(logits, bin_row, total_len)
    weights_local = lax.dynamic_slice_in_dim(weights_full, my_shard * local_rows, local_rows, 0)

    weighted = (weights_full[:, None] * cotangent[0].astype(jnp.float32)).astype(jnp.bfloat16)
    weighted = jnp.where(classify, jnp.zeros_like(weighted), weighted)
    grad = weight_grad_rows(normed, weighted.T, total_len ** (-0.5))
    return (weights_local[None, :], grad[None])


def solution(mesh):
    in_specs = (
        P("grp", "fsdp", None),
        P("grp", None),
        P("grp", None, "fsdp"),
        P("grp", "fsdp"),
        P("grp", None),
        P("grp", "fsdp"),
        P(),
        P("grp", None, "fsdp"),
    )
    out_specs = (P("grp", "fsdp"), P("grp", None, "fsdp"))
    return jax.shard_map(
        per_device, mesh=mesh, in_specs=in_specs, out_specs=out_specs, check_vma=False
    )
```

```python
import jax
import jax.numpy as jnp
from jax import lax
from jax.sharding import PartitionSpec as P
from jax.experimental import pallas as pl
from jax.experimental.pallas import tpu as pltpu

NBINS = 16
PROJ_ROWS = 256


def _project_kernel(rows_ref, weight_ref, out_ref):
    out_ref[...] = jnp.dot(
        rows_ref[...], weight_ref[...], preferred_element_type=jnp.float32
    ).astype(out_ref.dtype)


def project_rows(rows, weight):
    n_rows, depth = rows.shape
    width = weight.shape[1]
    return pl.pallas_call(
        _project_kernel,
        out_shape=jax.ShapeDtypeStruct((n_rows, width), jnp.bfloat16),
        grid=(n_rows // PROJ_ROWS,),
        in_specs=[
            pl.BlockSpec((PROJ_ROWS, depth), lambda i: (i, 0)),
            pl.BlockSpec((depth, width), lambda i: (0, 0)),
        ],
        out_specs=pl.BlockSpec((PROJ_ROWS, width), lambda i: (i, 0)),
        compiler_params=pltpu.CompilerParams(vmem_limit_bytes=48 * 1024 * 1024),
        cost_estimate=pl.CostEstimate(
            flops=2 * n_rows * depth * width,
            bytes_accessed=2 * (n_rows * depth + depth * width + n_rows * width),
            transcendentals=0,
        ),
    )(rows, weight)


def _normalize_kernel(rows_ref, scale_ref, out_ref):
    values_f = rows_ref[...].astype(jnp.float32)
    mean_sq = jnp.mean(values_f * values_f, axis=-1, keepdims=True)
    out_ref[...] = (values_f * lax.rsqrt(mean_sq + 1e-05) * scale_ref[...]).astype(out_ref.dtype)


def normalize_rows(rows_in, scale_row):
    return pl.pallas_call(
        _normalize_kernel,
        out_shape=jax.ShapeDtypeStruct(rows_in.shape, jnp.bfloat16),
        cost_estimate=pl.CostEstimate(
            flops=4 * rows_in.size, bytes_accessed=4 * rows_in.size, transcendentals=rows_in.shape[0]
        ),
    )(rows_in, scale_row[None, :])


def segment_ids(length_row, total_len):
    response_ends = jnp.cumsum(length_row)
    positions = jnp.arange(total_len, dtype=jnp.int32)
    return jnp.sum((positions[:, None] >= response_ends[None, :]).astype(jnp.int32), axis=1)


def head_logits(query_rows, key_rows, value_rows, score_row, segment):
    row_count = query_rows.shape[0]
    head_size = query_rows.shape[1]
    scores = jnp.dot(query_rows, key_rows.T, preferred_element_type=jnp.float32) * head_size ** (
        -0.5
    )
    query_pos = jnp.arange(row_count, dtype=jnp.int32)
    key_pos = jnp.arange(key_rows.shape[0], dtype=jnp.int32)
    allowed = (segment[:, None] == segment[None, :]) & (key_pos[None, :] <= query_pos[:, None])
    scores = jnp.where(allowed, scores, -1e30)
    highest = jnp.max(scores, axis=1, keepdims=True)
    expo = jnp.exp(scores - highest)
    weights = (expo / jnp.sum(expo, axis=1, keepdims=True)).astype(jnp.bfloat16)
    value_score = jnp.dot(
        value_rows.astype(jnp.float32), score_row, precision=lax.Precision.HIGHEST
    )
    return jnp.sum(weights.astype(jnp.float32) * value_score[None, :], axis=1)


GRAD_COLS = 1024


def _grad_kernel(scale, weighted_t_ref, rows_ref, out_ref):
    product = jnp.dot(weighted_t_ref[...], rows_ref[...], preferred_element_type=jnp.float32)
    out_ref[...] = (product * scale).T.astype(out_ref.dtype)


def weight_grad_rows(rows, weighted_t, scale):
    n_rows, depth = rows.shape
    width = weighted_t.shape[0]
    return pl.pallas_call(
        lambda *refs: _grad_kernel(scale, *refs),
        out_shape=jax.ShapeDtypeStruct((depth, width), jnp.bfloat16),
        grid=(depth // GRAD_COLS,),
        in_specs=[
            pl.BlockSpec((width, n_rows), lambda i: (0, 0)),
            pl.BlockSpec((n_rows, GRAD_COLS), lambda i: (0, i)),
        ],
        out_specs=pl.BlockSpec((GRAD_COLS, width), lambda i: (i, 0)),
        compiler_params=pltpu.CompilerParams(vmem_limit_bytes=48 * 1024 * 1024),
        cost_estimate=pl.CostEstimate(
            flops=2 * n_rows * depth * width,
            bytes_accessed=2 * (n_rows * depth + n_rows * width + depth * width),
            transcendentals=0,
        ),
    )(weighted_t, rows)


def group_weights(logits, bin_row, total_len):
    onehot = (bin_row[:, None] == jnp.arange(NBINS, dtype=jnp.int32)[None, :]).astype(jnp.float32)
    counts = jnp.sum(onehot, axis=0)
    sums = jnp.dot(jax.nn.sigmoid(logits), onehot, precision=lax.Precision.HIGHEST)
    calib = (counts - sums + 1.0) / (sums + 1.0)
    ratio = jnp.exp(logits) * jnp.dot(onehot, calib, precision=lax.Precision.HIGHEST)
    return ratio * total_len / jnp.sum(ratio)


def per_device(
    layer_input, norm_gain, layer_weight, score_vec, lengths, bins, group_map, cotangent
):
    n_groups = lax.axis_size("grp")
    half_groups = n_groups // 2
    my_group = lax.axis_index("grp")
    classify = my_group < half_groups
    normed = lax.all_gather(
        normalize_rows(layer_input[0], norm_gain[0]), "fsdp", axis=0, tiled=True
    )
    total_len = normed.shape[0]
    head_size = layer_weight.shape[2] // 3
    segment = segment_ids(lengths[0], total_len)
    score_row = score_vec[0].astype(jnp.float32)
    local_rows = bins.shape[1]

    def attend():
        projected = project_rows(normed, layer_weight[0])
        return head_logits(
            projected[:, :head_size],
            projected[:, head_size : 2 * head_size],
            projected[:, 2 * head_size :],
            score_row,
            segment,
        )

    def skipped():
        return jnp.zeros((total_len,), jnp.float32)

    contrib = lax.cond(classify, attend, skipped)
    my_shard = lax.axis_index("fsdp")
    n_shards = lax.axis_size("fsdp")
    bins_spread = lax.dynamic_update_slice_in_dim(
        jnp.zeros((total_len,), jnp.float32), bins[0].astype(jnp.float32), my_shard * local_rows, 0
    )
    packed = jnp.stack([contrib, bins_spread])
    step = 1
    while step < n_shards:
        packed = packed + lax.ppermute(
            packed, "fsdp", [(i, i ^ step) for i in range(n_shards)]
        )
        step *= 2
    policy_index = jnp.clip(my_group - half_groups, 0, half_groups - 1)
    source = group_map[policy_index]
    pick = (policy_index - source) % half_groups
    relayed = jnp.zeros_like(packed)
    for shift in range(half_groups):
        moved = lax.ppermute(
            packed,
            "grp",
            [(g, half_groups + (g + shift) % half_groups) for g in range(half_groups)],
        )
        relayed = jnp.where(pick == shift, moved, relayed)
    chosen = jnp.where(classify, packed, relayed)
    logits = chosen[0]
    bin_row = chosen[1].astype(jnp.int32)
    weights_full = group_weights(logits, bin_row, total_len)
    weights_local = lax.dynamic_slice_in_dim(weights_full, my_shard * local_rows, local_rows, 0)

    weighted = (weights_full[:, None] * cotangent[0].astype(jnp.float32)).astype(jnp.bfloat16)
    weighted = jnp.where(classify, jnp.zeros_like(weighted), weighted)
    grad = weight_grad_rows(normed, weighted.T, total_len ** (-0.5))
    return (weights_local[None, :], grad[None])


def solution(mesh):
    in_specs = (
        P("grp", "fsdp", None),
        P("grp", None),
        P("grp", None, "fsdp"),
        P("grp", "fsdp"),
        P("grp", None),
        P("grp", "fsdp"),
        P(),
        P("grp", None, "fsdp"),
    )
    out_specs = (P("grp", "fsdp"), P("grp", None, "fsdp"))
    return jax.shard_map(
        per_device, mesh=mesh, in_specs=in_specs, out_specs=out_specs, check_vma=False
    )
```

```python
import jax
import jax.numpy as jnp
from jax import lax
from jax.sharding import PartitionSpec as P
from jax.experimental import pallas as pl
from jax.experimental.pallas import tpu as pltpu

NBINS = 16
PROJ_ROWS = 512


def _project_kernel(rows_ref, weight_ref, out_ref):
    out_ref[...] = jnp.dot(
        rows_ref[...], weight_ref[...], preferred_element_type=jnp.float32
    ).astype(out_ref.dtype)


def project_rows(rows, weight):
    n_rows, depth = rows.shape
    width = weight.shape[1]
    return pl.pallas_call(
        _project_kernel,
        out_shape=jax.ShapeDtypeStruct((n_rows, width), jnp.bfloat16),
        grid=(n_rows // PROJ_ROWS,),
        in_specs=[
            pl.BlockSpec((PROJ_ROWS, depth), lambda i: (i, 0)),
            pl.BlockSpec((depth, width), lambda i: (0, 0)),
        ],
        out_specs=pl.BlockSpec((PROJ_ROWS, width), lambda i: (i, 0)),
        compiler_params=pltpu.CompilerParams(vmem_limit_bytes=48 * 1024 * 1024),
        cost_estimate=pl.CostEstimate(
            flops=2 * n_rows * depth * width,
            bytes_accessed=2 * (n_rows * depth + depth * width + n_rows * width),
            transcendentals=0,
        ),
    )(rows, weight)


def _normalize_kernel(rows_ref, scale_ref, out_ref):
    values_f = rows_ref[...].astype(jnp.float32)
    mean_sq = jnp.mean(values_f * values_f, axis=-1, keepdims=True)
    out_ref[...] = (values_f * lax.rsqrt(mean_sq + 1e-05) * scale_ref[...]).astype(out_ref.dtype)


def normalize_rows(rows_in, scale_row):
    return pl.pallas_call(
        _normalize_kernel,
        out_shape=jax.ShapeDtypeStruct(rows_in.shape, jnp.bfloat16),
        cost_estimate=pl.CostEstimate(
            flops=4 * rows_in.size, bytes_accessed=4 * rows_in.size, transcendentals=rows_in.shape[0]
        ),
    )(rows_in, scale_row[None, :])


def segment_ids(length_row, total_len):
    response_ends = jnp.cumsum(length_row)
    positions = jnp.arange(total_len, dtype=jnp.int32)
    return jnp.sum((positions[:, None] >= response_ends[None, :]).astype(jnp.int32), axis=1)


def head_logits(query_rows, key_rows, value_rows, score_row, segment):
    row_count = query_rows.shape[0]
    head_size = query_rows.shape[1]
    scores = jnp.dot(query_rows, key_rows.T, preferred_element_type=jnp.float32) * head_size ** (
        -0.5
    )
    query_pos = jnp.arange(row_count, dtype=jnp.int32)
    key_pos = jnp.arange(key_rows.shape[0], dtype=jnp.int32)
    allowed = (segment[:, None] == segment[None, :]) & (key_pos[None, :] <= query_pos[:, None])
    scores = jnp.where(allowed, scores, -1e30)
    highest = jnp.max(scores, axis=1, keepdims=True)
    expo = jnp.exp(scores - highest)
    weights = (expo / jnp.sum(expo, axis=1, keepdims=True)).astype(jnp.bfloat16)
    mixed = jnp.dot(weights, value_rows, preferred_element_type=jnp.float32)
    return jnp.dot(mixed, score_row, precision=lax.Precision.HIGHEST)


GRAD_COLS = 2048


def _grad_kernel(scale, weighted_t_ref, rows_ref, out_ref):
    product = jnp.dot(weighted_t_ref[...], rows_ref[...], preferred_element_type=jnp.float32)
    out_ref[...] = (product * scale).T.astype(out_ref.dtype)


def weight_grad_rows(rows, weighted_t, scale):
    n_rows, depth = rows.shape
    width = weighted_t.shape[0]
    return pl.pallas_call(
        lambda *refs: _grad_kernel(scale, *refs),
        out_shape=jax.ShapeDtypeStruct((depth, width), jnp.bfloat16),
        grid=(depth // GRAD_COLS,),
        in_specs=[
            pl.BlockSpec((width, n_rows), lambda i: (0, 0)),
            pl.BlockSpec((n_rows, GRAD_COLS), lambda i: (0, i)),
        ],
        out_specs=pl.BlockSpec((GRAD_COLS, width), lambda i: (i, 0)),
        compiler_params=pltpu.CompilerParams(vmem_limit_bytes=48 * 1024 * 1024),
        cost_estimate=pl.CostEstimate(
            flops=2 * n_rows * depth * width,
            bytes_accessed=2 * (n_rows * depth + n_rows * width + depth * width),
            transcendentals=0,
        ),
    )(weighted_t, rows)


def group_weights(logits, bin_row, total_len):
    onehot = (bin_row[:, None] == jnp.arange(NBINS, dtype=jnp.int32)[None, :]).astype(jnp.float32)
    counts = jnp.sum(onehot, axis=0)
    sums = jnp.dot(jax.nn.sigmoid(logits), onehot, precision=lax.Precision.HIGHEST)
    calib = (counts - sums + 1.0) / (sums + 1.0)
    ratio = jnp.exp(logits) * jnp.dot(onehot, calib, precision=lax.Precision.HIGHEST)
    return ratio * total_len / jnp.sum(ratio)


def per_device(
    layer_input, norm_gain, layer_weight, score_vec, lengths, bins, group_map, cotangent
):
    n_groups = lax.axis_size("grp")
    half_groups = n_groups // 2
    my_group = lax.axis_index("grp")
    classify = my_group < half_groups
    normed = lax.all_gather(
        normalize_rows(layer_input[0], norm_gain[0]), "fsdp", axis=0, tiled=True
    )
    total_len = normed.shape[0]
    head_size = layer_weight.shape[2] // 3
    segment = segment_ids(lengths[0], total_len)
    score_row = score_vec[0].astype(jnp.float32)
    local_rows = bins.shape[1]

    def attend():
        projected = project_rows(normed, layer_weight[0])
        return head_logits(
            projected[:, :head_size],
            projected[:, head_size : 2 * head_size],
            projected[:, 2 * head_size :],
            score_row,
            segment,
        )

    def skipped():
        return jnp.zeros((total_len,), jnp.float32)

    contrib = lax.cond(classify, attend, skipped)
    my_shard = lax.axis_index("fsdp")
    n_shards = lax.axis_size("fsdp")
    bins_spread = lax.dynamic_update_slice_in_dim(
        jnp.zeros((total_len,), jnp.float32), bins[0].astype(jnp.float32), my_shard * local_rows, 0
    )
    packed = jnp.stack([contrib, bins_spread])
    step = 1
    while step < n_shards:
        packed = packed + lax.ppermute(
            packed, "fsdp", [(i, i ^ step) for i in range(n_shards)]
        )
        step *= 2
    policy_index = jnp.clip(my_group - half_groups, 0, half_groups - 1)
    source = group_map[policy_index]
    pick = (policy_index - source) % half_groups
    relayed = jnp.zeros_like(packed)
    for shift in range(half_groups):
        moved = lax.ppermute(
            packed,
            "grp",
            [(g, half_groups + (g + shift) % half_groups) for g in range(half_groups)],
        )
        relayed = jnp.where(pick == shift, moved, relayed)
    chosen = jnp.where(classify, packed, relayed)
    logits = chosen[0]
    bin_row = chosen[1].astype(jnp.int32)
    weights_full = group_weights(logits, bin_row, total_len)
    weights_local = lax.dynamic_slice_in_dim(weights_full, my_shard * local_rows, local_rows, 0)

    weighted = (weights_full[:, None] * cotangent[0].astype(jnp.float32)).astype(jnp.bfloat16)
    weighted = jnp.where(classify, jnp.zeros_like(weighted), weighted)
    grad = weight_grad_rows(normed, weighted.T, total_len ** (-0.5))
    return (weights_local[None, :], grad[None])


def solution(mesh):
    in_specs = (
        P("grp", "fsdp", None),
        P("grp", None),
        P("grp", None, "fsdp"),
        P("grp", "fsdp"),
        P("grp", None),
        P("grp", "fsdp"),
        P(),
        P("grp", None, "fsdp"),
    )
    out_specs = (P("grp", "fsdp"), P("grp", None, "fsdp"))
    return jax.shard_map(
        per_device, mesh=mesh, in_specs=in_specs, out_specs=out_specs, check_vma=False
    )
```

```python
import jax
import jax.numpy as jnp
from jax import lax
from jax.sharding import PartitionSpec as P
from jax.experimental import pallas as pl
from jax.experimental.pallas import tpu as pltpu

NBINS = 16
PROJ_ROWS = 256


def _project_kernel(rows_ref, weight_ref, out_ref):
    out_ref[...] = jnp.dot(
        rows_ref[...], weight_ref[...], preferred_element_type=jnp.float32
    ).astype(out_ref.dtype)


def project_rows(rows, weight):
    n_rows, depth = rows.shape
    width = weight.shape[1]
    return pl.pallas_call(
        _project_kernel,
        out_shape=jax.ShapeDtypeStruct((n_rows, width), jnp.bfloat16),
        grid=(n_rows // PROJ_ROWS,),
        in_specs=[
            pl.BlockSpec((PROJ_ROWS, depth), lambda i: (i, 0)),
            pl.BlockSpec((depth, width), lambda i: (0, 0)),
        ],
        out_specs=pl.BlockSpec((PROJ_ROWS, width), lambda i: (i, 0)),
        compiler_params=pltpu.CompilerParams(vmem_limit_bytes=48 * 1024 * 1024),
        cost_estimate=pl.CostEstimate(
            flops=2 * n_rows * depth * width,
            bytes_accessed=2 * (n_rows * depth + depth * width + n_rows * width),
            transcendentals=0,
        ),
    )(rows, weight)


def _normalize_kernel(rows_ref, scale_ref, out_ref):
    values_f = rows_ref[...].astype(jnp.float32)
    mean_sq = jnp.mean(values_f * values_f, axis=-1, keepdims=True)
    out_ref[...] = (values_f * lax.rsqrt(mean_sq + 1e-05) * scale_ref[...]).astype(out_ref.dtype)


def normalize_rows(rows_in, scale_row):
    return pl.pallas_call(
        _normalize_kernel,
        out_shape=jax.ShapeDtypeStruct(rows_in.shape, jnp.bfloat16),
        cost_estimate=pl.CostEstimate(
            flops=4 * rows_in.size, bytes_accessed=4 * rows_in.size, transcendentals=rows_in.shape[0]
        ),
    )(rows_in, scale_row[None, :])


def segment_ids(length_row, total_len):
    response_ends = jnp.cumsum(length_row)
    positions = jnp.arange(total_len, dtype=jnp.int32)
    return jnp.sum((positions[:, None] >= response_ends[None, :]).astype(jnp.int32), axis=1)


def head_logits(query_rows, key_rows, value_rows, score_row, segment):
    row_count = query_rows.shape[0]
    head_size = query_rows.shape[1]
    scores = jnp.dot(query_rows, key_rows.T, preferred_element_type=jnp.float32) * head_size ** (
        -0.5
    )
    query_pos = jnp.arange(row_count, dtype=jnp.int32)
    key_pos = jnp.arange(key_rows.shape[0], dtype=jnp.int32)
    allowed = (segment[:, None] == segment[None, :]) & (key_pos[None, :] <= query_pos[:, None])
    scores = jnp.where(allowed, scores, -1e30)
    highest = jnp.max(scores, axis=1, keepdims=True)
    expo = jnp.exp(scores - highest)
    weights = (expo / jnp.sum(expo, axis=1, keepdims=True)).astype(jnp.bfloat16)
    mixed = jnp.dot(weights, value_rows, preferred_element_type=jnp.float32)
    return jnp.dot(mixed, score_row, precision=lax.Precision.HIGHEST)


GRAD_COLS = 2048


def _grad_kernel(scale, weighted_t_ref, rows_ref, out_ref):
    product = jnp.dot(weighted_t_ref[...], rows_ref[...], preferred_element_type=jnp.float32)
    out_ref[...] = (product * scale).T.astype(out_ref.dtype)


def weight_grad_rows(rows, weighted_t, scale):
    n_rows, depth = rows.shape
    width = weighted_t.shape[0]
    return pl.pallas_call(
        lambda *refs: _grad_kernel(scale, *refs),
        out_shape=jax.ShapeDtypeStruct((depth, width), jnp.bfloat16),
        grid=(depth // GRAD_COLS,),
        in_specs=[
            pl.BlockSpec((width, n_rows), lambda i: (0, 0)),
            pl.BlockSpec((n_rows, GRAD_COLS), lambda i: (0, i)),
        ],
        out_specs=pl.BlockSpec((GRAD_COLS, width), lambda i: (i, 0)),
        compiler_params=pltpu.CompilerParams(vmem_limit_bytes=48 * 1024 * 1024),
        cost_estimate=pl.CostEstimate(
            flops=2 * n_rows * depth * width,
            bytes_accessed=2 * (n_rows * depth + n_rows * width + depth * width),
            transcendentals=0,
        ),
    )(weighted_t, rows)


def group_weights(logits, bin_row, total_len):
    onehot = (bin_row[:, None] == jnp.arange(NBINS, dtype=jnp.int32)[None, :]).astype(jnp.float32)
    counts = jnp.sum(onehot, axis=0)
    sums = jnp.dot(jax.nn.sigmoid(logits), onehot, precision=lax.Precision.HIGHEST)
    calib = (counts - sums + 1.0) / (sums + 1.0)
    ratio = jnp.exp(logits) * jnp.dot(onehot, calib, precision=lax.Precision.HIGHEST)
    return ratio * total_len / jnp.sum(ratio)


def per_device(
    layer_input, norm_gain, layer_weight, score_vec, lengths, bins, group_map, cotangent
):
    n_groups = lax.axis_size("grp")
    half_groups = n_groups // 2
    my_group = lax.axis_index("grp")
    classify = my_group < half_groups
    normed = lax.all_gather(
        normalize_rows(layer_input[0], norm_gain[0]), "fsdp", axis=0, tiled=True
    )
    total_len = normed.shape[0]
    head_size = layer_weight.shape[2] // 3
    segment = segment_ids(lengths[0], total_len)
    score_row = score_vec[0].astype(jnp.float32)
    local_rows = bins.shape[1]

    def attend():
        projected = project_rows(normed, layer_weight[0])
        return head_logits(
            projected[:, :head_size],
            projected[:, head_size : 2 * head_size],
            projected[:, 2 * head_size :],
            score_row,
            segment,
        )

    def skipped():
        return jnp.zeros((total_len,), jnp.float32)

    contrib = lax.cond(classify, attend, skipped)
    my_shard = lax.axis_index("fsdp")
    n_shards = lax.axis_size("fsdp")
    bins_spread = lax.dynamic_update_slice_in_dim(
        jnp.zeros((total_len,), jnp.float32), bins[0].astype(jnp.float32), my_shard * local_rows, 0
    )
    packed = jnp.stack([contrib, bins_spread])
    step = 1
    while step < n_shards:
        packed = packed + lax.ppermute(
            packed, "fsdp", [(i, i ^ step) for i in range(n_shards)]
        )
        step *= 2
    policy_index = jnp.clip(my_group - half_groups, 0, half_groups - 1)
    source = group_map[policy_index]
    pick = (policy_index - source) % half_groups
    relayed = jnp.zeros_like(packed)
    for shift in range(half_groups):
        moved = lax.ppermute(
            packed,
            "grp",
            [(g, half_groups + (g + shift) % half_groups) for g in range(half_groups)],
        )
        relayed = jnp.where(pick == shift, moved, relayed)
    chosen = jnp.where(classify, packed, relayed)
    logits = chosen[0]
    bin_row = chosen[1].astype(jnp.int32)
    weights_full = group_weights(logits, bin_row, total_len)
    weights_local = lax.dynamic_slice_in_dim(weights_full, my_shard * local_rows, local_rows, 0)

    weighted = (weights_full[:, None] * cotangent[0].astype(jnp.float32)).astype(jnp.bfloat16)
    weighted = jnp.where(classify, jnp.zeros_like(weighted), weighted)
    grad = weight_grad_rows(normed, weighted.T, total_len ** (-0.5))
    return (weights_local[None, :], grad[None])


def solution(mesh):
    in_specs = (
        P("grp", "fsdp", None),
        P("grp", None),
        P("grp", None, "fsdp"),
        P("grp", "fsdp"),
        P("grp", None),
        P("grp", "fsdp"),
        P(),
        P("grp", None, "fsdp"),
    )
    out_specs = (P("grp", "fsdp"), P("grp", None, "fsdp"))
    return jax.shard_map(
        per_device, mesh=mesh, in_specs=in_specs, out_specs=out_specs, check_vma=False
    )
```

```python
import jax
import jax.numpy as jnp
from jax import lax
from jax.sharding import PartitionSpec as P
from jax.experimental import pallas as pl
from jax.experimental.pallas import tpu as pltpu

NBINS = 16
PROJ_ROWS = 256


def _project_kernel(rows_ref, weight_ref, out_ref):
    out_ref[...] = jnp.dot(
        rows_ref[...], weight_ref[...], preferred_element_type=jnp.float32
    ).astype(out_ref.dtype)


def project_rows(rows, weight):
    n_rows, depth = rows.shape
    width = weight.shape[1]
    return pl.pallas_call(
        _project_kernel,
        out_shape=jax.ShapeDtypeStruct((n_rows, width), jnp.bfloat16),
        grid=(n_rows // PROJ_ROWS,),
        in_specs=[
            pl.BlockSpec((PROJ_ROWS, depth), lambda i: (i, 0)),
            pl.BlockSpec((depth, width), lambda i: (0, 0)),
        ],
        out_specs=pl.BlockSpec((PROJ_ROWS, width), lambda i: (i, 0)),
        compiler_params=pltpu.CompilerParams(vmem_limit_bytes=48 * 1024 * 1024),
        cost_estimate=pl.CostEstimate(
            flops=2 * n_rows * depth * width,
            bytes_accessed=2 * (n_rows * depth + depth * width + n_rows * width),
            transcendentals=0,
        ),
    )(rows, weight)


def _normalize_kernel(rows_ref, scale_ref, out_ref):
    values_f = rows_ref[...].astype(jnp.float32)
    mean_sq = jnp.mean(values_f * values_f, axis=-1, keepdims=True)
    out_ref[...] = (values_f * lax.rsqrt(mean_sq + 1e-05) * scale_ref[...]).astype(out_ref.dtype)


def normalize_rows(rows_in, scale_row):
    return pl.pallas_call(
        _normalize_kernel,
        out_shape=jax.ShapeDtypeStruct(rows_in.shape, jnp.bfloat16),
        cost_estimate=pl.CostEstimate(
            flops=4 * rows_in.size, bytes_accessed=4 * rows_in.size, transcendentals=rows_in.shape[0]
        ),
    )(rows_in, scale_row[None, :])


def segment_ids(length_row, total_len):
    response_ends = jnp.cumsum(length_row)
    positions = jnp.arange(total_len, dtype=jnp.int32)
    return jnp.sum((positions[:, None] >= response_ends[None, :]).astype(jnp.int32), axis=1)


def head_logits(query_rows, key_rows, value_rows, score_row, segment):
    row_count = query_rows.shape[0]
    head_size = query_rows.shape[1]
    scores = jnp.dot(query_rows, key_rows.T, preferred_element_type=jnp.float32) * head_size ** (
        -0.5
    )
    query_pos = jnp.arange(row_count, dtype=jnp.int32)
    key_pos = jnp.arange(key_rows.shape[0], dtype=jnp.int32)
    allowed = (segment[:, None] == segment[None, :]) & (key_pos[None, :] <= query_pos[:, None])
    scores = jnp.where(allowed, scores, -1e30)
    highest = jnp.max(scores, axis=1, keepdims=True)
    expo = jnp.exp(scores - highest)
    weights = (expo / jnp.sum(expo, axis=1, keepdims=True)).astype(jnp.bfloat16)
    mixed = jnp.dot(weights, value_rows, preferred_element_type=jnp.float32)
    return jnp.dot(mixed, score_row, precision=lax.Precision.HIGHEST)


GRAD_COLS = 4096


def _grad_kernel(scale, weighted_t_ref, rows_ref, out_ref):
    product = jnp.dot(weighted_t_ref[...], rows_ref[...], preferred_element_type=jnp.float32)
    out_ref[...] = (product * scale).T.astype(out_ref.dtype)


def weight_grad_rows(rows, weighted_t, scale):
    n_rows, depth = rows.shape
    width = weighted_t.shape[0]
    return pl.pallas_call(
        lambda *refs: _grad_kernel(scale, *refs),
        out_shape=jax.ShapeDtypeStruct((depth, width), jnp.bfloat16),
        grid=(depth // GRAD_COLS,),
        in_specs=[
            pl.BlockSpec((width, n_rows), lambda i: (0, 0)),
            pl.BlockSpec((n_rows, GRAD_COLS), lambda i: (0, i)),
        ],
        out_specs=pl.BlockSpec((GRAD_COLS, width), lambda i: (i, 0)),
        compiler_params=pltpu.CompilerParams(vmem_limit_bytes=48 * 1024 * 1024),
        cost_estimate=pl.CostEstimate(
            flops=2 * n_rows * depth * width,
            bytes_accessed=2 * (n_rows * depth + n_rows * width + depth * width),
            transcendentals=0,
        ),
    )(weighted_t, rows)


def group_weights(logits, bin_row, total_len):
    onehot = (bin_row[:, None] == jnp.arange(NBINS, dtype=jnp.int32)[None, :]).astype(jnp.float32)
    counts = jnp.sum(onehot, axis=0)
    sums = jnp.dot(jax.nn.sigmoid(logits), onehot, precision=lax.Precision.HIGHEST)
    calib = (counts - sums + 1.0) / (sums + 1.0)
    ratio = jnp.exp(logits) * jnp.dot(onehot, calib, precision=lax.Precision.HIGHEST)
    return ratio * total_len / jnp.sum(ratio)


def per_device(
    layer_input, norm_gain, layer_weight, score_vec, lengths, bins, group_map, cotangent
):
    n_groups = lax.axis_size("grp")
    half_groups = n_groups // 2
    my_group = lax.axis_index("grp")
    classify = my_group < half_groups
    normed = lax.all_gather(
        normalize_rows(layer_input[0], norm_gain[0]), "fsdp", axis=0, tiled=True
    )
    total_len = normed.shape[0]
    head_size = layer_weight.shape[2] // 3
    segment = segment_ids(lengths[0], total_len)
    score_row = score_vec[0].astype(jnp.float32)
    local_rows = bins.shape[1]

    def attend():
        projected = project_rows(normed, layer_weight[0])
        return head_logits(
            projected[:, :head_size],
            projected[:, head_size : 2 * head_size],
            projected[:, 2 * head_size :],
            score_row,
            segment,
        )

    def skipped():
        return jnp.zeros((total_len,), jnp.float32)

    contrib = lax.cond(classify, attend, skipped)
    my_shard = lax.axis_index("fsdp")
    n_shards = lax.axis_size("fsdp")
    bins_spread = lax.dynamic_update_slice_in_dim(
        jnp.zeros((total_len,), jnp.float32), bins[0].astype(jnp.float32), my_shard * local_rows, 0
    )
    packed = jnp.stack([contrib, bins_spread])
    step = 1
    while step < n_shards:
        packed = packed + lax.ppermute(
            packed, "fsdp", [(i, i ^ step) for i in range(n_shards)]
        )
        step *= 2
    policy_index = jnp.clip(my_group - half_groups, 0, half_groups - 1)
    source = group_map[policy_index]
    pick = (policy_index - source) % half_groups
    relayed = jnp.zeros_like(packed)
    for shift in range(half_groups):
        moved = lax.ppermute(
            packed,
            "grp",
            [(g, half_groups + (g + shift) % half_groups) for g in range(half_groups)],
        )
        relayed = jnp.where(pick == shift, moved, relayed)
    chosen = jnp.where(classify, packed, relayed)
    logits = chosen[0]
    bin_row = chosen[1].astype(jnp.int32)
    weights_full = group_weights(logits, bin_row, total_len)
    weights_local = lax.dynamic_slice_in_dim(weights_full, my_shard * local_rows, local_rows, 0)

    weighted = (weights_full[:, None] * cotangent[0].astype(jnp.float32)).astype(jnp.bfloat16)
    weighted = jnp.where(classify, jnp.zeros_like(weighted), weighted)
    grad = weight_grad_rows(normed, weighted.T, total_len ** (-0.5))
    return (weights_local[None, :], grad[None])


def solution(mesh):
    in_specs = (
        P("grp", "fsdp", None),
        P("grp", None),
        P("grp", None, "fsdp"),
        P("grp", "fsdp"),
        P("grp", None),
        P("grp", "fsdp"),
        P(),
        P("grp", None, "fsdp"),
    )
    out_specs = (P("grp", "fsdp"), P("grp", None, "fsdp"))
    return jax.shard_map(
        per_device, mesh=mesh, in_specs=in_specs, out_specs=out_specs, check_vma=False
    )
```

```python
import jax
import jax.numpy as jnp
from jax import lax
from jax.sharding import PartitionSpec as P
from jax.experimental import pallas as pl
from jax.experimental.pallas import tpu as pltpu

NBINS = 16
PROJ_ROWS = 128


def _project_kernel(rows_ref, weight_ref, out_ref):
    out_ref[...] = jnp.dot(
        rows_ref[...], weight_ref[...], preferred_element_type=jnp.float32
    ).astype(out_ref.dtype)


def project_rows(rows, weight):
    n_rows, depth = rows.shape
    width = weight.shape[1]
    return pl.pallas_call(
        _project_kernel,
        out_shape=jax.ShapeDtypeStruct((n_rows, width), jnp.bfloat16),
        grid=(n_rows // PROJ_ROWS,),
        in_specs=[
            pl.BlockSpec((PROJ_ROWS, depth), lambda i: (i, 0)),
            pl.BlockSpec((depth, width), lambda i: (0, 0)),
        ],
        out_specs=pl.BlockSpec((PROJ_ROWS, width), lambda i: (i, 0)),
        compiler_params=pltpu.CompilerParams(vmem_limit_bytes=48 * 1024 * 1024),
        cost_estimate=pl.CostEstimate(
            flops=2 * n_rows * depth * width,
            bytes_accessed=2 * (n_rows * depth + depth * width + n_rows * width),
            transcendentals=0,
        ),
    )(rows, weight)


def _normalize_kernel(rows_ref, scale_ref, out_ref):
    values_f = rows_ref[...].astype(jnp.float32)
    mean_sq = jnp.mean(values_f * values_f, axis=-1, keepdims=True)
    out_ref[...] = (values_f * lax.rsqrt(mean_sq + 1e-05) * scale_ref[...]).astype(out_ref.dtype)


def normalize_rows(rows_in, scale_row):
    return pl.pallas_call(
        _normalize_kernel,
        out_shape=jax.ShapeDtypeStruct(rows_in.shape, jnp.bfloat16),
        cost_estimate=pl.CostEstimate(
            flops=4 * rows_in.size, bytes_accessed=4 * rows_in.size, transcendentals=rows_in.shape[0]
        ),
    )(rows_in, scale_row[None, :])


def segment_ids(length_row, total_len):
    response_ends = jnp.cumsum(length_row)
    positions = jnp.arange(total_len, dtype=jnp.int32)
    return jnp.sum((positions[:, None] >= response_ends[None, :]).astype(jnp.int32), axis=1)


def head_logits(query_rows, key_rows, value_rows, score_row, segment):
    row_count = query_rows.shape[0]
    head_size = query_rows.shape[1]
    scores = jnp.dot(query_rows, key_rows.T, preferred_element_type=jnp.float32) * head_size ** (
        -0.5
    )
    query_pos = jnp.arange(row_count, dtype=jnp.int32)
    key_pos = jnp.arange(key_rows.shape[0], dtype=jnp.int32)
    allowed = (segment[:, None] == segment[None, :]) & (key_pos[None, :] <= query_pos[:, None])
    scores = jnp.where(allowed, scores, -1e30)
    highest = jnp.max(scores, axis=1, keepdims=True)
    expo = jnp.exp(scores - highest)
    weights = (expo / jnp.sum(expo, axis=1, keepdims=True)).astype(jnp.bfloat16)
    mixed = jnp.dot(weights, value_rows, preferred_element_type=jnp.float32)
    return jnp.dot(mixed, score_row, precision=lax.Precision.HIGHEST)


GRAD_COLS = 2048


def _grad_kernel(scale, weighted_t_ref, rows_ref, out_ref):
    product = jnp.dot(weighted_t_ref[...], rows_ref[...], preferred_element_type=jnp.float32)
    out_ref[...] = (product * scale).T.astype(out_ref.dtype)


def weight_grad_rows(rows, weighted_t, scale):
    n_rows, depth = rows.shape
    width = weighted_t.shape[0]
    return pl.pallas_call(
        lambda *refs: _grad_kernel(scale, *refs),
        out_shape=jax.ShapeDtypeStruct((depth, width), jnp.bfloat16),
        grid=(depth // GRAD_COLS,),
        in_specs=[
            pl.BlockSpec((width, n_rows), lambda i: (0, 0)),
            pl.BlockSpec((n_rows, GRAD_COLS), lambda i: (0, i)),
        ],
        out_specs=pl.BlockSpec((GRAD_COLS, width), lambda i: (i, 0)),
        compiler_params=pltpu.CompilerParams(vmem_limit_bytes=48 * 1024 * 1024),
        cost_estimate=pl.CostEstimate(
            flops=2 * n_rows * depth * width,
            bytes_accessed=2 * (n_rows * depth + n_rows * width + depth * width),
            transcendentals=0,
        ),
    )(weighted_t, rows)


def group_weights(logits, bin_row, total_len):
    onehot = (bin_row[:, None] == jnp.arange(NBINS, dtype=jnp.int32)[None, :]).astype(jnp.float32)
    counts = jnp.sum(onehot, axis=0)
    sums = jnp.dot(jax.nn.sigmoid(logits), onehot, precision=lax.Precision.HIGHEST)
    calib = (counts - sums + 1.0) / (sums + 1.0)
    ratio = jnp.exp(logits) * jnp.dot(onehot, calib, precision=lax.Precision.HIGHEST)
    return ratio * total_len / jnp.sum(ratio)


def per_device(
    layer_input, norm_gain, layer_weight, score_vec, lengths, bins, group_map, cotangent
):
    n_groups = lax.axis_size("grp")
    half_groups = n_groups // 2
    my_group = lax.axis_index("grp")
    classify = my_group < half_groups
    normed = lax.all_gather(
        normalize_rows(layer_input[0], norm_gain[0]), "fsdp", axis=0, tiled=True
    )
    total_len = normed.shape[0]
    head_size = layer_weight.shape[2] // 3
    segment = segment_ids(lengths[0], total_len)
    score_row = score_vec[0].astype(jnp.float32)
    local_rows = bins.shape[1]

    def attend():
        projected = project_rows(normed, layer_weight[0])
        return head_logits(
            projected[:, :head_size],
            projected[:, head_size : 2 * head_size],
            projected[:, 2 * head_size :],
            score_row,
            segment,
        )

    def skipped():
        return jnp.zeros((total_len,), jnp.float32)

    contrib = lax.cond(classify, attend, skipped)
    my_shard = lax.axis_index("fsdp")
    n_shards = lax.axis_size("fsdp")
    bins_spread = lax.dynamic_update_slice_in_dim(
        jnp.zeros((total_len,), jnp.float32), bins[0].astype(jnp.float32), my_shard * local_rows, 0
    )
    packed = jnp.stack([contrib, bins_spread])
    step = 1
    while step < n_shards:
        packed = packed + lax.ppermute(
            packed, "fsdp", [(i, i ^ step) for i in range(n_shards)]
        )
        step *= 2
    policy_index = jnp.clip(my_group - half_groups, 0, half_groups - 1)
    source = group_map[policy_index]
    pick = (policy_index - source) % half_groups
    relayed = jnp.zeros_like(packed)
    for shift in range(half_groups):
        moved = lax.ppermute(
            packed,
            "grp",
            [(g, half_groups + (g + shift) % half_groups) for g in range(half_groups)],
        )
        relayed = jnp.where(pick == shift, moved, relayed)
    chosen = jnp.where(classify, packed, relayed)
    logits = chosen[0]
    bin_row = chosen[1].astype(jnp.int32)
    weights_full = group_weights(logits, bin_row, total_len)
    weights_local = lax.dynamic_slice_in_dim(weights_full, my_shard * local_rows, local_rows, 0)

    weighted = (weights_full[:, None] * cotangent[0].astype(jnp.float32)).astype(jnp.bfloat16)
    weighted = jnp.where(classify, jnp.zeros_like(weighted), weighted)
    grad = weight_grad_rows(normed, weighted.T, total_len ** (-0.5))
    return (weights_local[None, :], grad[None])


def solution(mesh):
    in_specs = (
        P("grp", "fsdp", None),
        P("grp", None),
        P("grp", None, "fsdp"),
        P("grp", "fsdp"),
        P("grp", None),
        P("grp", "fsdp"),
        P(),
        P("grp", None, "fsdp"),
    )
    out_specs = (P("grp", "fsdp"), P("grp", None, "fsdp"))
    return jax.shard_map(
        per_device, mesh=mesh, in_specs=in_specs, out_specs=out_specs, check_vma=False
    )
```
